256 devices in a mesh: orient: 16 (over y, x_lo, core), strip: 16 (over x_hi, z).
Axes of the slice: x: 4 (x_hi: 2, x_lo: 2; x = x_hi * 2 + x_lo), y: 4, z: 8, core: 2. Of those that a mesh axis runs over, the one named last changes fastest.
Arguments:
- inflow_field: bfloat16 [32, 8, 128, 512], P('orient', None, 'strip'), may hold values from -6 to 6
- kernel_one: bfloat16 [32, 9, 8, 8], replicated, may hold values from -0.125 to 0.125
- kernel_two: bfloat16 [32, 9, 8, 8], replicated, may hold values from -0.125 to 0.125
- turbine_mask: int32 [128, 512], P('strip'), may hold values 0 or 1
- wind_sector: int32 [1], replicated, may hold values from 0 to 31
- wake_cotangent: bfloat16 [32, 8, 128, 512], P('orient', None, 'strip'), may hold values from -6 to 6
Outputs:
- wake_out: bfloat16 [32, 8, 128, 512], P('orient', None, 'strip')
- kernel_grad_one: float32 [32, 9, 8, 8], replicated
- kernel_grad_two: float32 [32, 9, 8, 8], replicated
The draws below stay inside these ranges and needn't reach their ends.
Inputs may be any that keep to these rules, and one draw needn't show every extreme that they name: `wind_sector`: names one element of the group.
All inputs are finite; a program needn't handle non-finite values. No bound on the sum of `turbine_mask` on one device may be relied on, other than what follows from the above.
Results may differ from the reference program's by a relative error of at most 0.0051.
Values may be sent and summed in bfloat16 or wider, within the bound.
No kernel may reach another device: no remote copies, remote signals or barrier semaphores. Data moves between devices by JAX's collectives and lax.ppermute only.
A program may use at most 128 MiB of HBM per device.

```python
import math
import jax
import jax.numpy as jnp
from jax import lax

G = 32
CH = 8
TAPS = 9
COLS = 512
ROWS = 128


def touch_ends(array, rng, low, high):
    place = [jax.random.randint(jax.random.fold_in(rng, axis), (), 0, length) for axis, length in enumerate(array.shape)]
    main_axis = array.shape.index(max(array.shape))
    beside = place[:main_axis] + [(place[main_axis] + 1) % array.shape[main_axis]] + place[main_axis + 1:]
    return array.at[tuple(place)].set(low).at[tuple(beside)].set(high)


def level_of(own_key, dims, cuts, least, largest):
    level, own = 1.0, jax.random.fold_in(own_key, 6)
    for position, blocks in cuts:
        draws = jnp.exp(jax.random.uniform(jax.random.fold_in(own, position), (blocks,), jnp.float32, least / len(cuts), largest / len(cuts)))
        level = level * jnp.repeat(draws, dims[position] // blocks).reshape([-1 if axis == position else 1 for axis in range(len(dims))])
    return level


def normal_values(own_key, dims, scale, most, cuts=(), held_as=jnp.bfloat16):
    result = jax.random.normal(own_key, dims, jnp.float32) * scale
    if len(cuts) > 0:
        result = level_of(own_key, dims, cuts, -0.22, 0.18) * result
    return jnp.clip(result, min=-most, max=most).astype(held_as)


def setup_inputs(seed: int = 0) -> dict:
    key_of = jax.random.split(jax.random.key(seed), 7)
    return {
        "inflow_field": normal_values(key_of[0], (G, CH, ROWS, COLS), 1.0, 6.0, ((0, 16), (2, 16))),
        "kernel_one": normal_values(key_of[1], (G, TAPS, CH, CH), (G * TAPS * CH) ** -0.5, 0.125),
        "kernel_two": normal_values(key_of[2], (G, TAPS, CH, CH), (G * TAPS * CH) ** -0.5, 0.125),
        "turbine_mask": touch_ends((jax.random.randint(key_of[3], (ROWS, COLS), 0, 8) < 1).astype(jnp.int32), jax.random.fold_in(key_of[3], 1), 0, 1),
        "wind_sector": jax.random.randint(key_of[4], (1,), 0, G).astype(jnp.int32),
        "wake_cotangent": normal_values(key_of[5], (G, CH, ROWS, COLS), 1.0, 6.0, ((0, 16), (2, 16))),
    }


OFFSETS = ((0, 0), (0, 1), (0, 2), (1, 0), (1, 1), (1, 2), (2, 0), (2, 1), (2, 2))

def relative(row_ids, col_ids, sector):
    halfway = G // 2
    row_rot = row_ids % halfway
    row_ref = row_ids // halfway
    col_rot = col_ids % halfway
    col_ref = col_ids // halfway
    sec_rot = sector % halfway
    sec_ref = sector // halfway
    moved_rot = (sec_rot + (1 - 2 * sec_ref) * col_rot) % halfway
    moved_ref = (sec_ref + col_ref) % 2
    inverse_rot = jnp.where(row_ref == 0, (halfway - row_rot) % halfway, row_rot)
    result_rot = (inverse_rot + (1 - 2 * row_ref) * moved_rot) % halfway
    result_ref = (row_ref + moved_ref) % 2
    return (result_ref * halfway + result_rot).astype(jnp.int32)

def kernel_block(kernel, row_ids, col_ids, sector):
    channels = kernel.shape[2]
    tap_count = kernel.shape[1]
    relation = relative(row_ids[:, None], col_ids[None, :], sector).reshape(-1)
    onehot = (relation[:, None] == jnp.arange(G, dtype=jnp.int32)[None, :]).astype(jnp.bfloat16)
    picked = jnp.dot(onehot, kernel.reshape(G, -1), preferred_element_type=jnp.float32)
    picked = picked.reshape(row_ids.shape[0], col_ids.shape[0], tap_count, channels, channels)
    picked = picked.transpose(2, 0, 3, 1, 4)
    return picked.reshape(tap_count, row_ids.shape[0] * channels, col_ids.shape[0] * channels).astype(jnp.bfloat16)

def fold_kernel(partial_grad, row_ids, col_ids, sector):
    tap_count = partial_grad.shape[0]
    channels = partial_grad.shape[1] // row_ids.shape[0]
    relation = relative(row_ids[:, None], col_ids[None, :], sector).reshape(-1)
    onehot = (relation[:, None] == jnp.arange(G, dtype=jnp.int32)[None, :]).astype(jnp.float32)
    arranged = partial_grad.reshape(tap_count, row_ids.shape[0], channels, col_ids.shape[0], channels)
    arranged = arranged.transpose(1, 3, 0, 2, 4).reshape(relation.shape[0], -1)
    folded = jnp.dot(onehot.T, arranged, precision=lax.Precision.HIGHEST, preferred_element_type=jnp.float32)
    return folded.reshape(G, tap_count, channels, channels)

def conv_forward(source, weights):
    full_width, height, extent = source.shape
    padded = jnp.pad(source, ((0, 0), (1, 1), (1, 1)))
    summed = jnp.zeros((weights.shape[1], height * extent), jnp.float32)
    for tap_index, (row_shift, col_shift) in enumerate(OFFSETS):
        window = padded[:, row_shift:row_shift + height, col_shift:col_shift + extent].reshape(full_width, -1)
        summed = summed + jnp.dot(weights[tap_index], window, preferred_element_type=jnp.float32)
    return summed.reshape(-1, height, extent)

def conv_backward(gradient, weights):
    full_width, height, extent = gradient.shape
    padded = jnp.pad(gradient, ((0, 0), (1, 1), (1, 1)))
    summed = jnp.zeros((weights.shape[2], height * extent), jnp.float32)
    for tap_index, (row_shift, col_shift) in enumerate(OFFSETS):
        window = padded[:, 2 - row_shift:2 - row_shift + height, 2 - col_shift:2 - col_shift + extent].reshape(full_width, -1)
        summed = summed + jnp.dot(weights[tap_index].T, window, preferred_element_type=jnp.float32)
    return summed.reshape(-1, height, extent)

def weight_grad(gradient, source):
    full_width, height, extent = source.shape
    padded = jnp.pad(source, ((0, 0), (1, 1), (1, 1)))
    flat_grad = gradient.reshape(gradient.shape[0], -1)
    pieces = []
    for row_shift, col_shift in OFFSETS:
        window = padded[:, row_shift:row_shift + height, col_shift:col_shift + extent].reshape(full_width, -1)
        pieces.append(lax.dot_general(flat_grad, window, (((1,), (1,)), ((), ())), preferred_element_type=jnp.float32))
    return jnp.stack(pieces, 0)

def reference(inflow_field, kernel_one, kernel_two, turbine_mask, wind_sector, wake_cotangent):
    full_width = G * CH
    sector = wind_sector[0]
    neutral = jnp.int32(0)
    groups = jnp.arange(G, dtype=jnp.int32)
    weights_one = kernel_block(kernel_one, groups, groups, sector)
    weights_two = kernel_block(kernel_two, groups, groups, neutral)
    open_cells = (1 - turbine_mask).astype(jnp.float32)
    source = inflow_field.reshape(full_width, ROWS, COLS)
    first_pre = conv_forward(source, weights_one)
    sigmoid_one = jax.nn.sigmoid(first_pre)
    hidden = (first_pre * sigmoid_one * open_cells).astype(jnp.bfloat16)
    second_pre = conv_forward(hidden, weights_two)
    wake_out = second_pre.astype(jnp.bfloat16).reshape(G, CH, ROWS, COLS)
    cotangent = wake_cotangent.reshape(full_width, ROWS, COLS)
    scale_factor = 1.0 / math.sqrt(G * ROWS * COLS)
    grad_two = fold_kernel(weight_grad(cotangent, hidden), groups, groups, neutral) * scale_factor
    back_grad = conv_backward(cotangent, weights_two)
    first_grad = (back_grad * open_cells * sigmoid_one * (1.0 + first_pre * (1.0 - sigmoid_one))).astype(jnp.bfloat16)
    grad_one = fold_kernel(weight_grad(first_grad, source), groups, groups, sector) * scale_factor
    return (wake_out, grad_one, grad_two)
```

```python
import math

import jax
import jax.numpy as jnp
from jax import lax
from jax.sharding import PartitionSpec as P

G = 32


OFFSETS = ((0, 0), (0, 1), (0, 2), (1, 0), (1, 1), (1, 2), (2, 0), (2, 1), (2, 2))


def with_halo(shard, sides, width):
    for axis, dim in sides:
        count, length = (lax.axis_size(axis), shard.shape[dim])
        up = [(i, (i + 1) % count) for i in range(count - 1)]
        down = [(j, i) for i, j in up]
        last = lax.slice_in_dim(shard, length - width, length, axis=dim)
        first = lax.slice_in_dim(shard, 0, width, axis=dim)
        before = lax.ppermute(last, axis, up)
        after = lax.ppermute(first, axis, down)
        shard = jnp.concatenate([before, shard, after], axis=dim)
    return shard


def relative(row_ids, col_ids, sector):
    halfway = G // 2
    row_rot = row_ids % halfway
    row_ref = row_ids // halfway
    col_rot = col_ids % halfway
    col_ref = col_ids // halfway
    sec_rot = sector % halfway
    sec_ref = sector // halfway
    moved_rot = (sec_rot + (1 - 2 * sec_ref) * col_rot) % halfway
    moved_ref = (sec_ref + col_ref) % 2
    inverse_rot = jnp.where(row_ref == 0, (halfway - row_rot) % halfway, row_rot)
    result_rot = (inverse_rot + (1 - 2 * row_ref) * moved_rot) % halfway
    result_ref = (row_ref + moved_ref) % 2
    return result_ref * halfway + result_rot


def kernel_block(kernel, row_ids, col_ids, sector):
    channels = kernel.shape[2]
    tap_count = kernel.shape[1]
    relation = relative(row_ids[:, None], col_ids[None, :], sector).reshape(-1)
    onehot = (relation[:, None] == jnp.arange(G, dtype=jnp.int32)[None, :]).astype(jnp.bfloat16)
    picked = jnp.dot(onehot, kernel.reshape(G, -1), preferred_element_type=jnp.float32)
    picked = picked.reshape(row_ids.shape[0], col_ids.shape[0], tap_count, channels, channels)
    picked = picked.transpose(2, 0, 3, 1, 4)
    return picked.reshape(
        tap_count, row_ids.shape[0] * channels, col_ids.shape[0] * channels
    ).astype(jnp.bfloat16)


def fold_kernel(partial_grad, row_ids, col_ids, sector):
    tap_count = partial_grad.shape[0]
    channels = partial_grad.shape[1] // row_ids.shape[0]
    relation = relative(row_ids[:, None], col_ids[None, :], sector).reshape(-1)
    onehot = (relation[:, None] == jnp.arange(G, dtype=jnp.int32)[None, :]).astype(jnp.float32)
    arranged = partial_grad.reshape(
        tap_count, row_ids.shape[0], channels, col_ids.shape[0], channels
    )
    arranged = arranged.transpose(1, 3, 0, 2, 4).reshape(relation.shape[0], -1)
    folded = jnp.dot(
        onehot.T, arranged, precision=lax.Precision.HIGHEST, preferred_element_type=jnp.float32
    )
    return folded.reshape(G, tap_count, channels, channels)


def place_forward(mixed_taps, height, extent):
    padded = jnp.pad(mixed_taps, ((0, 0), (0, 0), (0, 0), (1, 1)))
    summed = jnp.zeros((mixed_taps.shape[1], height, extent), jnp.float32)
    for tap_index, (row_shift, col_shift) in enumerate(OFFSETS):
        summed = (
            summed
            + padded[tap_index, :, row_shift : row_shift + height, col_shift : col_shift + extent]
        )
    return summed


def place_backward(mixed_taps, height, extent):
    padded = jnp.pad(mixed_taps, ((0, 0), (0, 0), (0, 0), (1, 1)))
    summed = jnp.zeros((mixed_taps.shape[1], height, extent), jnp.float32)
    for tap_index, (row_shift, col_shift) in enumerate(OFFSETS):
        summed = (
            summed
            + padded[
                tap_index,
                :,
                2 - row_shift : 2 - row_shift + height,
                2 - col_shift : 2 - col_shift + extent,
            ]
        )
    return summed


def layer_forward(source, weights_row):
    tap_count, local_width, full_width = weights_row.shape
    height, extent = (source.shape[1], source.shape[2])
    matrix = weights_row.reshape(tap_count * local_width, full_width)
    widened = with_halo(source, (("strip", 1),), 1)
    gathered = lax.all_gather(widened, "orient", axis=0, tiled=True)
    mixed_taps = jnp.dot(
        matrix, gathered.reshape(full_width, -1), preferred_element_type=jnp.float32
    )
    mixed_taps = mixed_taps.reshape(tap_count, local_width, gathered.shape[1], extent)
    center = gathered[:, 1 : height + 1]
    return (place_forward(mixed_taps, height, extent), center)


def rim_rows(gradient):
    return with_halo(gradient, (("strip", 1),), 1)


def weight_grad(cot_rows, center):
    height, extent = (center.shape[1], center.shape[2])
    padded = jnp.pad(cot_rows, ((0, 0), (0, 0), (1, 1)))
    flat_center = center.reshape(center.shape[0], -1)
    pieces = []
    for row_shift, col_shift in OFFSETS:
        window = padded[
            :, 2 - row_shift : 2 - row_shift + height, 2 - col_shift : 2 - col_shift + extent
        ]
        window = window.reshape(cot_rows.shape[0], -1)
        pieces.append(
            lax.dot_general(
                window, flat_center, (((1,), (1,)), ((), ())), preferred_element_type=jnp.float32
            )
        )
    return jnp.stack(pieces, 0)


def all_sum(flat, axes):
    count = lax.axis_size(axes)
    parts = lax.all_to_all(flat.reshape(count, -1), axes, 0, 0, tiled=True).sum(0)
    spread = jnp.broadcast_to(parts[None], (count,) + parts.shape)
    return lax.all_to_all(spread, axes, 0, 0, tiled=True).reshape(-1)


def shards(inflow_field, kernel_one, kernel_two, turbine_mask, wind_sector, wake_cotangent):
    groups, channels, height, extent = inflow_field.shape
    local_width = groups * channels
    sector = wind_sector[0]
    neutral = jnp.int32(0)
    all_groups = jnp.arange(G, dtype=jnp.int32)
    scale_factor = 1.0 / math.sqrt(G * height * lax.axis_size("strip") * extent)
    first_group = lax.axis_index("orient") * groups
    my_groups = first_group + jnp.arange(groups, dtype=jnp.int32)
    row_one = kernel_block(kernel_one, my_groups, all_groups, sector)
    row_two = kernel_block(kernel_two, my_groups, all_groups, neutral)
    open_cells = (1 - turbine_mask).astype(jnp.float32)
    source = inflow_field.reshape(local_width, height, extent)
    first_pre, first_center = layer_forward(source, row_one)
    sigmoid_one = jax.nn.sigmoid(first_pre)
    hidden = (first_pre * sigmoid_one * open_cells).astype(jnp.bfloat16)
    second_pre, second_center = layer_forward(hidden, row_two)
    wake_out = second_pre.astype(jnp.bfloat16).reshape(groups, channels, height, extent)
    cotangent = wake_cotangent.reshape(local_width, height, extent)
    cot_two = rim_rows(cotangent)
    grad_two = weight_grad(cot_two, second_center)
    cot_all = lax.all_gather(cot_two, "orient", axis=0, tiled=True)
    col_two = kernel_block(kernel_two, all_groups, my_groups, neutral)
    cols_turned = col_two.transpose(0, 2, 1)
    mixed_taps = jnp.dot(
        cols_turned.reshape(9 * local_width, local_width * lax.axis_size("orient")),
        cot_all.reshape(local_width * lax.axis_size("orient"), -1),
        preferred_element_type=jnp.float32,
    )
    mixed_taps = mixed_taps.reshape(9, local_width, height + 2, extent)
    back_grad = place_backward(mixed_taps, height, extent)
    first_grad = (
        back_grad * open_cells * sigmoid_one * (1.0 + first_pre * (1.0 - sigmoid_one))
    ).astype(jnp.bfloat16)
    cot_one = rim_rows(first_grad)
    grad_one = weight_grad(cot_one, first_center)
    share_one = fold_kernel(grad_one, my_groups, all_groups, sector) * scale_factor
    share_two = fold_kernel(grad_two, my_groups, all_groups, neutral) * scale_factor
    flat = jnp.concatenate([share_one.reshape(-1), share_two.reshape(-1)])
    flat = all_sum(flat, ("orient", "strip"))
    summed_one, summed_two = jnp.split(flat, 2)
    summed_one = summed_one.reshape(share_one.shape)
    summed_two = summed_two.reshape(share_two.shape)
    return (wake_out, summed_one, summed_two)


def solution(mesh):
    return jax.shard_map(
        shards,
        mesh=mesh,
        in_specs=(
            P("orient", None, "strip", None),
            P(),
            P(),
            P("strip", None),
            P(),
            P("orient", None, "strip", None),
        ),
        out_specs=(P("orient", None, "strip", None), P(), P()),
        check_vma=False,
    )
```

```python
import math

import jax
import jax.numpy as jnp
from jax import lax
from jax.sharding import PartitionSpec as P

G = 32
TAPS = ((0, 0), (0, 1), (0, 2), (1, 0), (1, 1), (1, 2), (2, 0), (2, 1), (2, 2))


def relative(row_ids, col_ids, sector):
    halfway = G // 2
    row_rot = row_ids % halfway
    row_ref = row_ids // halfway
    col_rot = col_ids % halfway
    col_ref = col_ids // halfway
    sec_rot = sector % halfway
    sec_ref = sector // halfway
    moved_rot = (sec_rot + (1 - 2 * sec_ref) * col_rot) % halfway
    moved_ref = (sec_ref + col_ref) % 2
    inverse_rot = jnp.where(row_ref == 0, (halfway - row_rot) % halfway, row_rot)
    result_rot = (inverse_rot + (1 - 2 * row_ref) * moved_rot) % halfway
    result_ref = (row_ref + moved_ref) % 2
    return result_ref * halfway + result_rot


def relation_of(sector):
    ids = jnp.arange(G, dtype=jnp.int32)
    return relative(ids[:, None], ids[None, :], sector).reshape(-1)


def picked_of(kernel, relation):
    taps, channels = kernel.shape[1], kernel.shape[2]
    picked = jnp.take(kernel, relation, axis=0)
    return picked.reshape(G, G, taps, channels, channels)


def forward_matrix(picked):
    width = G * picked.shape[3]
    return picked.transpose(0, 3, 2, 1, 4).reshape(width, -1)


def backward_matrix(picked):
    width = G * picked.shape[3]
    return picked.transpose(1, 4, 2, 0, 3).reshape(width, -1)


def fold(flat_grad, relation, channels):
    taps = len(TAPS)
    arranged = flat_grad.reshape(G, channels, taps, G, channels)
    arranged = arranged.transpose(0, 3, 2, 1, 4).reshape(G * G, -1)
    onehot = (relation[:, None] == jnp.arange(G, dtype=jnp.int32)[None, :]).astype(jnp.float32)
    folded = jnp.dot(
        onehot.T, arranged, precision=lax.Precision.HIGHEST, preferred_element_type=jnp.float32
    )
    return folded.reshape(G, taps, channels, channels)


def windows(grid, height, extent, start=0):
    pieces = [
        grid[:, start + a : start + a + height, start + b : start + b + extent].reshape(grid.shape[0], -1)
        for a, b in TAPS
    ]
    return jnp.concatenate(pieces, axis=0)


def row_halo(block, width):
    count = lax.axis_size("strip")
    up = [(i, i + 1) for i in range(count - 1)]
    down = [(j, i) for i, j in up]
    length = block.shape[1]
    before = lax.ppermute(block[:, length - width :], "strip", up)
    after = lax.ppermute(block[:, :width], "strip", down)
    return jnp.concatenate([before, block, after], axis=1)


def all_sum(flat, axes):
    count = lax.axis_size(axes)
    parts = lax.all_to_all(flat.reshape(count, -1), axes, 0, 0, tiled=True).sum(0)
    spread = jnp.broadcast_to(parts[None], (count,) + parts.shape)
    return lax.all_to_all(spread, axes, 0, 0, tiled=True).reshape(-1)


def shards(inflow_field, kernel_one, kernel_two, turbine_mask, wind_sector, wake_cotangent):
    groups, channels, height, extent = inflow_field.shape
    local_width = groups * channels
    blocks = lax.axis_size("orient")
    span = extent // blocks
    scale_factor = 1.0 / math.sqrt(G * height * lax.axis_size("strip") * extent)
    sector = wind_sector[0]
    rel_one = relation_of(sector)
    rel_two = relation_of(jnp.int32(0))
    picked_one = picked_of(kernel_one, rel_one)
    picked_two = picked_of(kernel_two, rel_two)
    w_one = forward_matrix(picked_one)
    w_two = forward_matrix(picked_two)
    wt_two = backward_matrix(picked_two)

    open_cells = (1 - turbine_mask).astype(jnp.bfloat16)[None]
    stacked = jnp.concatenate(
        [
            inflow_field.reshape(local_width, height, extent),
            wake_cotangent.reshape(local_width, height, extent),
            open_cells,
        ],
        axis=0,
    )
    widened = row_halo(stacked, 2)
    widened = jnp.pad(widened, ((0, 0), (0, 0), (2, 2)))
    mine = lax.axis_index("orient")
    open_here = lax.dynamic_slice_in_dim(widened[2 * local_width :], mine * span, span + 4, axis=2)
    open_here = open_here[0].astype(jnp.float32)
    sending = jnp.stack(
        [widened[: 2 * local_width, :, j * span : j * span + span + 4] for j in range(blocks)], 0
    )
    arrived = lax.all_to_all(sending, "orient", 0, 0, tiled=True)
    full_width = blocks * local_width
    grid_rows, grid_cols = height + 4, span + 4
    source = arrived[:, :local_width].reshape(full_width, grid_rows, grid_cols)
    cotangent = arrived[:, local_width:].reshape(full_width, grid_rows, grid_cols)

    x_cols = windows(source, height + 2, span + 2)
    first_pre = jnp.dot(w_one, x_cols, preferred_element_type=jnp.float32)
    first_pre = first_pre.reshape(full_width, height + 2, span + 2)
    sigmoid_one = jax.nn.sigmoid(first_pre)
    hidden = (first_pre * sigmoid_one * open_here[None, 1:-1, 1:-1]).astype(jnp.bfloat16)

    h_cols = windows(hidden, height, span)
    second_pre = jnp.dot(w_two, h_cols, preferred_element_type=jnp.float32)
    wake = second_pre.astype(jnp.bfloat16).reshape(blocks, local_width, height, span)
    back = lax.all_to_all(wake, "orient", 0, 0, tiled=True)
    wake_out = back.transpose(1, 2, 0, 3).reshape(groups, channels, height, extent)

    cot_rim = cotangent[:, 1:-1, 1:-1]
    cot_mid = cotangent[:, 2:-2, 2:-2].reshape(full_width, -1)
    c_cols = jnp.concatenate(
        [
            cot_rim[:, 2 - a : 2 - a + height, 2 - b : 2 - b + span].reshape(full_width, -1)
            for a, b in TAPS
        ],
        axis=0,
    )
    back_grad = jnp.dot(wt_two, c_cols, preferred_element_type=jnp.float32)
    pre_mid = first_pre[:, 1:-1, 1:-1].reshape(full_width, -1)
    sig_mid = sigmoid_one[:, 1:-1, 1:-1].reshape(full_width, -1)
    open_mid = open_here[2:-2, 2:-2].reshape(1, -1)
    first_grad = (back_grad * open_mid * sig_mid * (1.0 + pre_mid * (1.0 - sig_mid))).astype(
        jnp.bfloat16
    )
    grad_two = lax.dot_general(
        cot_mid, h_cols, (((1,), (1,)), ((), ())), preferred_element_type=jnp.float32
    )
    x_mid = x_cols.reshape(-1, height + 2, span + 2)[:, 1:-1, 1:-1].reshape(x_cols.shape[0], -1)
    grad_one = lax.dot_general(
        first_grad, x_mid, (((1,), (1,)), ((), ())), preferred_element_type=jnp.float32
    )
    share_one = fold(grad_one, rel_one, channels) * scale_factor
    share_two = fold(grad_two, rel_two, channels) * scale_factor
    flat = jnp.concatenate([share_one.reshape(-1), share_two.reshape(-1)])
    flat = all_sum(flat, ("orient", "strip"))
    summed_one, summed_two = jnp.split(flat, 2)
    return (wake_out, summed_one.reshape(share_one.shape), summed_two.reshape(share_two.shape))


def solution(mesh):
    return jax.shard_map(
        shards,
        mesh=mesh,
        in_specs=(
            P("orient", None, "strip", None),
            P(),
            P(),
            P("strip", None),
            P(),
            P("orient", None, "strip", None),
        ),
        out_specs=(P("orient", None, "strip", None), P(), P()),
        check_vma=False,
    )
```

```python
import math

import jax
import jax.numpy as jnp
from jax import lax
from jax.sharding import PartitionSpec as P

G = 32
TAPS = ((0, 0), (0, 1), (0, 2), (1, 0), (1, 1), (1, 2), (2, 0), (2, 1), (2, 2))


def relative(row_ids, col_ids, sector):
    halfway = G // 2
    row_rot = row_ids % halfway
    row_ref = row_ids // halfway
    col_rot = col_ids % halfway
    col_ref = col_ids // halfway
    sec_rot = sector % halfway
    sec_ref = sector // halfway
    moved_rot = (sec_rot + (1 - 2 * sec_ref) * col_rot) % halfway
    moved_ref = (sec_ref + col_ref) % 2
    inverse_rot = jnp.where(row_ref == 0, (halfway - row_rot) % halfway, row_rot)
    result_rot = (inverse_rot + (1 - 2 * row_ref) * moved_rot) % halfway
    result_ref = (row_ref + moved_ref) % 2
    return result_ref * halfway + result_rot


def relation_of(sector):
    ids = jnp.arange(G, dtype=jnp.int32)
    return relative(ids[:, None], ids[None, :], sector).reshape(-1)


def forward_matrix(kernel, relation):
    taps, channels = kernel.shape[1], kernel.shape[2]
    onehot = (relation[:, None] == jnp.arange(G, dtype=jnp.int32)[None, :]).astype(kernel.dtype)
    moved = kernel.transpose(2, 0, 1, 3).reshape(channels, G, taps * channels)
    picked = jnp.einsum("xr,crm->cxm", onehot, moved, preferred_element_type=jnp.float32)
    picked = picked.astype(kernel.dtype).reshape(channels, G, G, taps * channels)
    return picked.transpose(1, 0, 2, 3).reshape(G * channels, -1)


def backward_matrix(kernel, relation):
    taps, channels = kernel.shape[1], kernel.shape[2]
    turned = relation.reshape(G, G).T.reshape(-1)
    onehot = (turned[:, None] == jnp.arange(G, dtype=jnp.int32)[None, :]).astype(kernel.dtype)
    moved = kernel.transpose(3, 0, 1, 2).reshape(channels, G, taps * channels)
    picked = jnp.einsum("xr,drm->dxm", onehot, moved, preferred_element_type=jnp.float32)
    picked = picked.astype(kernel.dtype).reshape(channels, G, G, taps * channels)
    return picked.transpose(1, 0, 2, 3).reshape(G * channels, -1)


def fold(flat_grad, relation, channels):
    taps = len(TAPS)
    arranged = flat_grad.reshape(G, channels, G, taps * channels).transpose(1, 0, 2, 3)
    arranged = arranged.reshape(channels, G * G, taps * channels)
    onehot = (relation[:, None] == jnp.arange(G, dtype=jnp.int32)[None, :]).astype(jnp.float32)
    folded = jnp.einsum(
        "xr,cxm->crm", onehot, arranged, precision=lax.Precision.HIGHEST,
        preferred_element_type=jnp.float32,
    )
    return folded.reshape(channels, G, taps, channels).transpose(1, 2, 0, 3)


def windows(grid, height, extent, start=0):
    channels = grid.shape[0] // G
    pieces = [
        grid[:, start + a : start + a + height, start + b : start + b + extent].reshape(G, channels, -1)
        for a, b in TAPS
    ]
    return jnp.stack(pieces, axis=1).reshape(grid.shape[0] * len(TAPS), -1)


def row_halo(block, width):
    count = lax.axis_size("strip")
    up = [(i, i + 1) for i in range(count - 1)]
    down = [(j, i) for i, j in up]
    length = block.shape[1]
    before = lax.ppermute(block[:, length - width :], "strip", up)
    after = lax.ppermute(block[:, :width], "strip", down)
    return jnp.concatenate([before, block, after], axis=1)


def all_sum(flat, axes):
    count = lax.axis_size(axes)
    parts = lax.all_to_all(flat.reshape(count, -1), axes, 0, 0, tiled=True).sum(0)
    spread = jnp.broadcast_to(parts[None], (count,) + parts.shape)
    return lax.all_to_all(spread, axes, 0, 0, tiled=True).reshape(-1)


def shards(inflow_field, kernel_one, kernel_two, turbine_mask, wind_sector, wake_cotangent):
    groups, channels, height, extent = inflow_field.shape
    local_width = groups * channels
    blocks = lax.axis_size("orient")
    span = extent // blocks
    scale_factor = 1.0 / math.sqrt(G * height * lax.axis_size("strip") * extent)
    sector = wind_sector[0]
    rel_one = relation_of(sector)
    rel_two = relation_of(jnp.int32(0))
    w_one = forward_matrix(kernel_one, rel_one)
    w_two = forward_matrix(kernel_two, rel_two)
    wt_two = backward_matrix(kernel_two, rel_two)

    open_cells = (1 - turbine_mask).astype(jnp.bfloat16)[None]
    stacked = jnp.concatenate(
        [
            inflow_field.reshape(local_width, height, extent),
            wake_cotangent.reshape(local_width, height, extent),
            open_cells,
        ],
        axis=0,
    )
    widened = row_halo(stacked, 2)
    widened = jnp.pad(widened, ((0, 0), (0, 0), (2, 2)))
    mine = lax.axis_index("orient")
    open_here = lax.dynamic_slice_in_dim(widened[2 * local_width :], mine * span, span + 4, axis=2)
    open_here = open_here[0].astype(jnp.float32)
    sending = jnp.stack(
        [widened[: 2 * local_width, :, j * span : j * span + span + 4] for j in range(blocks)], 0
    )
    arrived = lax.all_to_all(sending, "orient", 0, 0, tiled=True)
    full_width = blocks * local_width
    grid_rows, grid_cols = height + 4, span + 4
    source = arrived[:, :local_width].reshape(full_width, grid_rows, grid_cols)
    cotangent = arrived[:, local_width:].reshape(full_width, grid_rows, grid_cols)

    x_cols = windows(source, height + 2, span + 2)
    first_pre = jnp.dot(w_one, x_cols, preferred_element_type=jnp.float32)
    first_pre = first_pre.reshape(full_width, height + 2, span + 2)
    sigmoid_one = jax.nn.sigmoid(first_pre)
    hidden = (first_pre * sigmoid_one * open_here[None, 1:-1, 1:-1]).astype(jnp.bfloat16)

    h_cols = windows(hidden, height, span)
    second_pre = jnp.dot(w_two, h_cols, preferred_element_type=jnp.float32)
    wake = second_pre.astype(jnp.bfloat16).reshape(blocks, local_width, height, span)
    back = lax.all_to_all(wake, "orient", 0, 0, tiled=True)
    wake_out = back.transpose(1, 2, 0, 3).reshape(groups, channels, height, extent)

    cot_rim = cotangent[:, 1:-1, 1:-1]
    cot_mid = cotangent[:, 2:-2, 2:-2].reshape(full_width, -1)
    c_cols = jnp.stack(
        [
            cot_rim[:, 2 - a : 2 - a + height, 2 - b : 2 - b + span].reshape(G, channels, -1)
            for a, b in TAPS
        ],
        axis=1,
    ).reshape(full_width * len(TAPS), -1)
    back_grad = jnp.dot(wt_two, c_cols, preferred_element_type=jnp.float32)
    pre_mid = first_pre[:, 1:-1, 1:-1].reshape(full_width, -1)
    sig_mid = sigmoid_one[:, 1:-1, 1:-1].reshape(full_width, -1)
    open_mid = open_here[2:-2, 2:-2].reshape(1, -1)
    first_grad = (back_grad * open_mid * sig_mid * (1.0 + pre_mid * (1.0 - sig_mid))).astype(
        jnp.bfloat16
    )
    grad_two = lax.dot_general(
        cot_mid, h_cols, (((1,), (1,)), ((), ())), preferred_element_type=jnp.float32
    )
    x_mid = x_cols.reshape(x_cols.shape[0], height + 2, span + 2)[:, 1:-1, 1:-1].reshape(x_cols.shape[0], -1)
    grad_one = lax.dot_general(
        first_grad, x_mid, (((1,), (1,)), ((), ())), preferred_element_type=jnp.float32
    )
    share_one = fold(grad_one, rel_one, channels) * scale_factor
    share_two = fold(grad_two, rel_two, channels) * scale_factor
    flat = jnp.concatenate([share_one.reshape(-1), share_two.reshape(-1)])
    flat = all_sum(flat, ("orient", "strip"))
    summed_one, summed_two = jnp.split(flat, 2)
    return (wake_out, summed_one.reshape(share_one.shape), summed_two.reshape(share_two.shape))


def solution(mesh):
    return jax.shard_map(
        shards,
        mesh=mesh,
        in_specs=(
            P("orient", None, "strip", None),
            P(),
            P(),
            P("strip", None),
            P(),
            P("orient", None, "strip", None),
        ),
        out_specs=(P("orient", None, "strip", None), P(), P()),
        check_vma=False,
    )
```

```python
import math

import jax
import jax.numpy as jnp
from jax import lax
from jax.sharding import PartitionSpec as P

G = 32
TAPS = ((0, 0), (0, 1), (0, 2), (1, 0), (1, 1), (1, 2), (2, 0), (2, 1), (2, 2))


def relative(row_ids, col_ids, sector):
    halfway = G // 2
    row_rot = row_ids % halfway
    row_ref = row_ids // halfway
    col_rot = col_ids % halfway
    col_ref = col_ids // halfway
    sec_rot = sector % halfway
    sec_ref = sector // halfway
    moved_rot = (sec_rot + (1 - 2 * sec_ref) * col_rot) % halfway
    moved_ref = (sec_ref + col_ref) % 2
    inverse_rot = jnp.where(row_ref == 0, (halfway - row_rot) % halfway, row_rot)
    result_rot = (inverse_rot + (1 - 2 * row_ref) * moved_rot) % halfway
    result_ref = (row_ref + moved_ref) % 2
    return result_ref * halfway + result_rot


def relation_of(sector):
    ids = jnp.arange(G, dtype=jnp.int32)
    return relative(ids[:, None], ids[None, :], sector).reshape(-1)


def forward_matrix(kernel, relation):
    taps, channels = kernel.shape[1], kernel.shape[2]
    onehot = (relation[:, None] == jnp.arange(G, dtype=jnp.int32)[None, :]).astype(kernel.dtype)
    moved = kernel.transpose(2, 0, 1, 3).reshape(channels, G, taps * channels)
    picked = jnp.einsum("xr,crm->cxm", onehot, moved, preferred_element_type=jnp.float32)
    picked = picked.astype(kernel.dtype).reshape(channels, G, G, taps * channels)
    return picked.transpose(1, 0, 2, 3).reshape(G * channels, -1)


def backward_matrix(kernel, relation):
    taps, channels = kernel.shape[1], kernel.shape[2]
    turned = relation.reshape(G, G).T.reshape(-1)
    onehot = (turned[:, None] == jnp.arange(G, dtype=jnp.int32)[None, :]).astype(kernel.dtype)
    moved = kernel.transpose(3, 0, 1, 2).reshape(channels, G, taps * channels)
    picked = jnp.einsum("xr,drm->dxm", onehot, moved, preferred_element_type=jnp.float32)
    picked = picked.astype(kernel.dtype).reshape(channels, G, G, taps * channels)
    return picked.transpose(1, 0, 2, 3).reshape(G * channels, -1)


def fold(flat_grad, relation, channels):
    taps = len(TAPS)
    arranged = flat_grad.reshape(G, channels, G, taps * channels).transpose(1, 0, 2, 3)
    arranged = arranged.reshape(channels, G * G, taps * channels)
    onehot = (relation[:, None] == jnp.arange(G, dtype=jnp.int32)[None, :]).astype(jnp.float32)
    folded = jnp.einsum(
        "xr,cxm->crm", onehot, arranged, precision=lax.Precision.HIGHEST,
        preferred_element_type=jnp.float32,
    )
    return folded.reshape(channels, G, taps, channels).transpose(1, 2, 0, 3)


def windows(grid, height, extent, start=0):
    channels = grid.shape[0] // G
    pieces = [
        grid[:, start + a : start + a + height, start + b : start + b + extent].reshape(G, channels, -1)
        for a, b in TAPS
    ]
    return jnp.stack(pieces, axis=1).reshape(grid.shape[0] * len(TAPS), -1)


def flat_windows(flat, starts, length):
    channels = flat.shape[0] // G
    pieces = [flat[:, start : start + length].reshape(G, channels, length) for start in starts]
    return jnp.stack(pieces, axis=1).reshape(flat.shape[0] * len(TAPS), length)


def row_halo(block, width):
    count = lax.axis_size("strip")
    up = [(i, i + 1) for i in range(count - 1)]
    down = [(j, i) for i, j in up]
    length = block.shape[1]
    before = lax.ppermute(block[:, length - width :], "strip", up)
    after = lax.ppermute(block[:, :width], "strip", down)
    return jnp.concatenate([before, block, after], axis=1)


def all_sum(flat, axes):
    count = lax.axis_size(axes)
    parts = lax.all_to_all(flat.reshape(count, -1), axes, 0, 0, tiled=True).sum(0)
    spread = jnp.broadcast_to(parts[None], (count,) + parts.shape)
    return lax.all_to_all(spread, axes, 0, 0, tiled=True).reshape(-1)


def shards(inflow_field, kernel_one, kernel_two, turbine_mask, wind_sector, wake_cotangent):
    groups, channels, height, extent = inflow_field.shape
    local_width = groups * channels
    blocks = lax.axis_size("orient")
    span = extent // blocks
    scale_factor = 1.0 / math.sqrt(G * height * lax.axis_size("strip") * extent)
    sector = wind_sector[0]
    rel_one = relation_of(sector)
    rel_two = relation_of(jnp.int32(0))
    w_one = forward_matrix(kernel_one, rel_one)
    w_two = forward_matrix(kernel_two, rel_two)
    wt_two = backward_matrix(kernel_two, rel_two)

    open_cells = (1 - turbine_mask).astype(jnp.bfloat16)[None]
    stacked = jnp.concatenate(
        [
            inflow_field.reshape(local_width, height, extent),
            wake_cotangent.reshape(local_width, height, extent),
            open_cells,
        ],
        axis=0,
    )
    widened = row_halo(stacked, 2)
    widened = jnp.pad(widened, ((0, 0), (0, 0), (2, 2)))
    mine = lax.axis_index("orient")
    open_here = lax.dynamic_slice_in_dim(widened[2 * local_width :], mine * span, span + 4, axis=2)
    open_here = open_here[0].astype(jnp.float32)
    sending = jnp.stack(
        [widened[: 2 * local_width, :, j * span : j * span + span + 4] for j in range(blocks)], 0
    )
    arrived = lax.all_to_all(sending, "orient", 0, 0, tiled=True)
    full_width = blocks * local_width
    grid_rows, grid_cols = height + 4, span + 4
    source = arrived[:, :local_width].reshape(full_width, grid_rows, grid_cols)
    cotangent = arrived[:, local_width:].reshape(full_width, grid_rows, grid_cols)

    stride = grid_cols
    flat_source = jnp.pad(source.reshape(full_width, -1), ((0, 0), (0, 2)))
    flat_cot = cotangent.reshape(full_width, -1)
    rim_len = (height + 2) * stride
    mid_len = height * stride
    live = (jnp.arange(stride) < span).astype(jnp.float32)
    open_rim = jnp.pad(open_here[1:-1, 1:-1], ((0, 0), (0, 2))).reshape(1, -1)
    open_mid = (jnp.pad(open_here[2:-2, 2:-2], ((0, 0), (0, 4)))).reshape(1, -1)
    live_mid = jnp.broadcast_to(live[None], (height, stride)).reshape(1, -1)

    x_cols = flat_windows(flat_source, [a * stride + b for a, b in TAPS], rim_len)
    first_pre = jnp.dot(w_one, x_cols, preferred_element_type=jnp.float32)
    sigmoid_one = jax.nn.sigmoid(first_pre)
    hidden = (first_pre * sigmoid_one * open_rim).astype(jnp.bfloat16)

    flat_hidden = jnp.pad(hidden, ((0, 0), (0, 2)))
    h_cols = flat_windows(flat_hidden, [a * stride + b for a, b in TAPS], mid_len)
    second_pre = jnp.dot(w_two, h_cols, preferred_element_type=jnp.float32)
    wake = second_pre.reshape(full_width, height, stride)[:, :, :span].astype(jnp.bfloat16)
    wake = wake.reshape(blocks, local_width, height, span)
    back = lax.all_to_all(wake, "orient", 0, 0, tiled=True)
    wake_out = back.transpose(1, 2, 0, 3).reshape(groups, channels, height, extent)

    c_cols = flat_windows(flat_cot, [(3 - a) * stride + 3 - b for a, b in TAPS], mid_len)
    back_grad = jnp.dot(wt_two, c_cols, preferred_element_type=jnp.float32)
    pre_mid = first_pre[:, stride + 1 : stride + 1 + mid_len]
    sig_mid = sigmoid_one[:, stride + 1 : stride + 1 + mid_len]
    first_grad = (back_grad * open_mid * sig_mid * (1.0 + pre_mid * (1.0 - sig_mid))).astype(
        jnp.bfloat16
    )
    cot_mid = flat_cot[:, 2 * stride + 2 : 2 * stride + 2 + mid_len] * live_mid.astype(jnp.bfloat16)
    grad_two = lax.dot_general(
        cot_mid, h_cols, (((1,), (1,)), ((), ())), preferred_element_type=jnp.float32
    )
    x_mid = x_cols[:, stride + 1 : stride + 1 + mid_len]
    grad_one = lax.dot_general(
        first_grad, x_mid, (((1,), (1,)), ((), ())), preferred_element_type=jnp.float32
    )
    share_one = fold(grad_one, rel_one, channels) * scale_factor
    share_two = fold(grad_two, rel_two, channels) * scale_factor
    flat = jnp.concatenate([share_one.reshape(-1), share_two.reshape(-1)])
    flat = all_sum(flat, ("orient", "strip"))
    summed_one, summed_two = jnp.split(flat, 2)
    return (wake_out, summed_one.reshape(share_one.shape), summed_two.reshape(share_two.shape))


def solution(mesh):
    return jax.shard_map(
        shards,
        mesh=mesh,
        in_specs=(
            P("orient", None, "strip", None),
            P(),
            P(),
            P("strip", None),
            P(),
            P("orient", None, "strip", None),
        ),
        out_specs=(P("orient", None, "strip", None), P(), P()),
        check_vma=False,
    )
```

```python
import math

import jax
import jax.numpy as jnp
from jax import lax
from jax.sharding import PartitionSpec as P

G = 32
TAPS = ((0, 0), (0, 1), (0, 2), (1, 0), (1, 1), (1, 2), (2, 0), (2, 1), (2, 2))


def relative(row_ids, col_ids, sector):
    halfway = G // 2
    row_rot = row_ids % halfway
    row_ref = row_ids // halfway
    col_rot = col_ids % halfway
    col_ref = col_ids // halfway
    sec_rot = sector % halfway
    sec_ref = sector // halfway
    moved_rot = (sec_rot + (1 - 2 * sec_ref) * col_rot) % halfway
    moved_ref = (sec_ref + col_ref) % 2
    inverse_rot = jnp.where(row_ref == 0, (halfway - row_rot) % halfway, row_rot)
    result_rot = (inverse_rot + (1 - 2 * row_ref) * moved_rot) % halfway
    result_ref = (row_ref + moved_ref) % 2
    return result_ref * halfway + result_rot


def relation_of(sector):
    ids = jnp.arange(G, dtype=jnp.int32)
    return relative(ids[:, None], ids[None, :], sector).reshape(-1)


SLOTS = 16


def padded_taps(kernel):
    return jnp.pad(kernel, ((0, 0), (0, SLOTS - kernel.shape[1]), (0, 0), (0, 0)))


def forward_matrix(kernel, relation):
    channels = kernel.shape[2]
    onehot = (relation[:, None] == jnp.arange(G, dtype=jnp.int32)[None, :]).astype(kernel.dtype)
    moved = padded_taps(kernel).transpose(2, 0, 1, 3).reshape(channels, G, SLOTS * channels)
    picked = jnp.einsum("xr,crm->cxm", onehot, moved, preferred_element_type=jnp.float32)
    picked = picked.astype(kernel.dtype).reshape(channels, G, G, SLOTS * channels)
    return picked.transpose(1, 0, 2, 3).reshape(G * channels, -1)


def backward_matrix(kernel, relation):
    channels = kernel.shape[2]
    turned = relation.reshape(G, G).T.reshape(-1)
    onehot = (turned[:, None] == jnp.arange(G, dtype=jnp.int32)[None, :]).astype(kernel.dtype)
    moved = padded_taps(kernel).transpose(3, 0, 1, 2).reshape(channels, G, SLOTS * channels)
    picked = jnp.einsum("xr,drm->dxm", onehot, moved, preferred_element_type=jnp.float32)
    picked = picked.astype(kernel.dtype).reshape(channels, G, G, SLOTS * channels)
    return picked.transpose(1, 0, 2, 3).reshape(G * channels, -1)


def fold(flat_grad, relation, channels):
    taps = len(TAPS)
    arranged = flat_grad.reshape(G, channels, G, SLOTS * channels).transpose(1, 0, 2, 3)
    arranged = arranged.reshape(channels, G * G, SLOTS * channels)
    onehot = (relation[:, None] == jnp.arange(G, dtype=jnp.int32)[None, :]).astype(jnp.float32)
    folded = jnp.einsum(
        "xr,cxm->crm", onehot, arranged, precision=lax.Precision.HIGHEST,
        preferred_element_type=jnp.float32,
    )
    folded = folded.reshape(channels, G, SLOTS, channels)[:, :, :taps]
    return folded.transpose(1, 2, 0, 3)


def flat_windows(flat, starts, length):
    channels = flat.shape[0] // G
    pieces = [flat[:, start : start + length].reshape(G, channels, length) for start in starts]
    blank = jnp.zeros_like(pieces[0])
    pieces = pieces + [blank] * (SLOTS - len(pieces))
    return jnp.stack(pieces, axis=1).reshape(flat.shape[0] * SLOTS, length)


def row_halo(block, width):
    count = lax.axis_size("strip")
    up = [(i, i + 1) for i in range(count - 1)]
    down = [(j, i) for i, j in up]
    length = block.shape[1]
    before = lax.ppermute(block[:, length - width :], "strip", up)
    after = lax.ppermute(block[:, :width], "strip", down)
    return jnp.concatenate([before, block, after], axis=1)


def all_sum(flat, axes):
    count = lax.axis_size(axes)
    parts = lax.all_to_all(flat.reshape(count, -1), axes, 0, 0, tiled=True).sum(0)
    spread = jnp.broadcast_to(parts[None], (count,) + parts.shape)
    return lax.all_to_all(spread, axes, 0, 0, tiled=True).reshape(-1)


def shards(inflow_field, kernel_one, kernel_two, turbine_mask, wind_sector, wake_cotangent):
    groups, channels, height, extent = inflow_field.shape
    local_width = groups * channels
    blocks = lax.axis_size("orient")
    span = extent // blocks
    scale_factor = 1.0 / math.sqrt(G * height * lax.axis_size("strip") * extent)
    sector = wind_sector[0]
    rel_one = relation_of(sector)
    rel_two = relation_of(jnp.int32(0))
    w_one = forward_matrix(kernel_one, rel_one)
    w_two = forward_matrix(kernel_two, rel_two)
    wt_two = backward_matrix(kernel_two, rel_two)

    open_cells = (1 - turbine_mask).astype(jnp.bfloat16)[None]
    stacked = jnp.concatenate(
        [
            inflow_field.reshape(local_width, height, extent),
            wake_cotangent.reshape(local_width, height, extent),
            open_cells,
        ],
        axis=0,
    )
    widened = row_halo(stacked, 2)
    widened = jnp.pad(widened, ((0, 0), (0, 0), (2, 2)))
    mine = lax.axis_index("orient")
    open_here = lax.dynamic_slice_in_dim(widened[2 * local_width :], mine * span, span + 4, axis=2)
    open_here = open_here[0].astype(jnp.float32)
    sending = jnp.stack(
        [widened[: 2 * local_width, :, j * span : j * span + span + 4] for j in range(blocks)], 0
    )
    arrived = lax.all_to_all(sending, "orient", 0, 0, tiled=True)
    full_width = blocks * local_width
    grid_rows, grid_cols = height + 4, span + 4
    source = arrived[:, :local_width].reshape(full_width, grid_rows, grid_cols)
    cotangent = arrived[:, local_width:].reshape(full_width, grid_rows, grid_cols)

    stride = grid_cols
    flat_source = jnp.pad(source.reshape(full_width, -1), ((0, 0), (0, 2)))
    flat_cot = cotangent.reshape(full_width, -1)
    rim_len = (height + 2) * stride
    mid_len = height * stride
    live = (jnp.arange(stride) < span).astype(jnp.float32)
    open_rim = jnp.pad(open_here[1:-1, 1:-1], ((0, 0), (0, 2))).reshape(1, -1)
    open_mid = (jnp.pad(open_here[2:-2, 2:-2], ((0, 0), (0, 4)))).reshape(1, -1)
    live_mid = jnp.broadcast_to(live[None], (height, stride)).reshape(1, -1)

    x_cols = flat_windows(flat_source, [a * stride + b for a, b in TAPS], rim_len)
    first_pre = jnp.dot(w_one, x_cols, preferred_element_type=jnp.float32)
    sigmoid_one = jax.nn.sigmoid(first_pre)
    hidden = (first_pre * sigmoid_one * open_rim).astype(jnp.bfloat16)

    flat_hidden = jnp.pad(hidden, ((0, 0), (0, 2)))
    h_cols = flat_windows(flat_hidden, [a * stride + b for a, b in TAPS], mid_len)
    second_pre = jnp.dot(w_two, h_cols, preferred_element_type=jnp.float32)
    wake = second_pre.reshape(full_width, height, stride)[:, :, :span].astype(jnp.bfloat16)
    wake = wake.reshape(blocks, local_width, height, span)
    back = lax.all_to_all(wake, "orient", 0, 0, tiled=True)
    wake_out = back.transpose(1, 2, 0, 3).reshape(groups, channels, height, extent)

    c_cols = flat_windows(flat_cot, [(3 - a) * stride + 3 - b for a, b in TAPS], mid_len)
    back_grad = jnp.dot(wt_two, c_cols, preferred_element_type=jnp.float32)
    pre_mid = first_pre[:, stride + 1 : stride + 1 + mid_len]
    sig_mid = sigmoid_one[:, stride + 1 : stride + 1 + mid_len]
    first_grad = (back_grad * open_mid * sig_mid * (1.0 + pre_mid * (1.0 - sig_mid))).astype(
        jnp.bfloat16
    )
    cot_mid = flat_cot[:, 2 * stride + 2 : 2 * stride + 2 + mid_len] * live_mid.astype(jnp.bfloat16)
    grad_two = lax.dot_general(
        cot_mid, h_cols, (((1,), (1,)), ((), ())), preferred_element_type=jnp.float32
    )
    x_mid = x_cols[:, stride + 1 : stride + 1 + mid_len]
    grad_one = lax.dot_general(
        first_grad, x_mid, (((1,), (1,)), ((), ())), preferred_element_type=jnp.float32
    )
    share_one = fold(grad_one, rel_one, channels) * scale_factor
    share_two = fold(grad_two, rel_two, channels) * scale_factor
    flat = jnp.concatenate([share_one.reshape(-1), share_two.reshape(-1)])
    flat = all_sum(flat, ("orient", "strip"))
    summed_one, summed_two = jnp.split(flat, 2)
    return (wake_out, summed_one.reshape(share_one.shape), summed_two.reshape(share_two.shape))


def solution(mesh):
    return jax.shard_map(
        shards,
        mesh=mesh,
        in_specs=(
            P("orient", None, "strip", None),
            P(),
            P(),
            P("strip", None),
            P(),
            P("orient", None, "strip", None),
        ),
        out_specs=(P("orient", None, "strip", None), P(), P()),
        check_vma=False,
    )
```

```python
import math

import jax
import jax.numpy as jnp
from jax import lax
from jax.sharding import PartitionSpec as P

G = 32
TAPS = ((0, 0), (0, 1), (0, 2), (1, 0), (1, 1), (1, 2), (2, 0), (2, 1), (2, 2))


def relative(row_ids, col_ids, sector):
    halfway = G // 2
    row_rot = row_ids % halfway
    row_ref = row_ids // halfway
    col_rot = col_ids % halfway
    col_ref = col_ids // halfway
    sec_rot = sector % halfway
    sec_ref = sector // halfway
    moved_rot = (sec_rot + (1 - 2 * sec_ref) * col_rot) % halfway
    moved_ref = (sec_ref + col_ref) % 2
    inverse_rot = jnp.where(row_ref == 0, (halfway - row_rot) % halfway, row_rot)
    result_rot = (inverse_rot + (1 - 2 * row_ref) * moved_rot) % halfway
    result_ref = (row_ref + moved_ref) % 2
    return result_ref * halfway + result_rot


def relation_of(sector):
    ids = jnp.arange(G, dtype=jnp.int32)
    return relative(ids[:, None], ids[None, :], sector).reshape(-1)


def forward_matrix(kernel, relation):
    taps, channels = kernel.shape[1], kernel.shape[2]
    onehot = (relation[:, None] == jnp.arange(G, dtype=jnp.int32)[None, :]).astype(kernel.dtype)
    moved = kernel.transpose(2, 0, 1, 3).reshape(channels, G, taps * channels)
    picked = jnp.einsum("xr,crm->cxm", onehot, moved, preferred_element_type=jnp.float32)
    picked = picked.astype(kernel.dtype).reshape(channels, G, G, taps * channels)
    return picked.transpose(1, 0, 2, 3).reshape(G * channels, -1)


def backward_matrix(kernel, relation):
    taps, channels = kernel.shape[1], kernel.shape[2]
    turned = relation.reshape(G, G).T.reshape(-1)
    onehot = (turned[:, None] == jnp.arange(G, dtype=jnp.int32)[None, :]).astype(kernel.dtype)
    moved = kernel.transpose(3, 0, 1, 2).reshape(channels, G, taps * channels)
    picked = jnp.einsum("xr,drm->dxm", onehot, moved, preferred_element_type=jnp.float32)
    picked = picked.astype(kernel.dtype).reshape(channels, G, G, taps * channels)
    return picked.transpose(1, 0, 2, 3).reshape(G * channels, -1)


def fold(flat_grad, relation, channels):
    taps = len(TAPS)
    arranged = flat_grad.reshape(G, channels, G, taps * channels).transpose(1, 0, 2, 3)
    arranged = arranged.reshape(channels, G * G, taps * channels)
    onehot = (relation[:, None] == jnp.arange(G, dtype=jnp.int32)[None, :]).astype(jnp.float32)
    folded = jnp.einsum(
        "xr,cxm->crm", onehot, arranged, precision=lax.Precision.HIGHEST,
        preferred_element_type=jnp.float32,
    )
    return folded.reshape(channels, G, taps, channels).transpose(1, 2, 0, 3)


def windows(grid, height, extent, start=0):
    channels = grid.shape[0] // G
    pieces = [
        grid[:, start + a : start + a + height, start + b : start + b + extent].reshape(G, channels, -1)
        for a, b in TAPS
    ]
    return jnp.stack(pieces, axis=1).reshape(grid.shape[0] * len(TAPS), -1)


def flat_windows(flat, starts, length):
    channels = flat.shape[0] // G
    pieces = [flat[:, start : start + length].reshape(G, channels, length) for start in starts]
    return jnp.stack(pieces, axis=1).reshape(flat.shape[0] * len(TAPS), length)


def row_halo(block, width):
    count = lax.axis_size("strip")
    up = [(i, i + 1) for i in range(count - 1)]
    down = [(j, i) for i, j in up]
    length = block.shape[1]
    before = lax.ppermute(block[:, length - width :], "strip", up)
    after = lax.ppermute(block[:, :width], "strip", down)
    return jnp.concatenate([before, block, after], axis=1)


def all_sum(flat, axes):
    count = lax.axis_size(axes)
    parts = lax.all_to_all(flat.reshape(count, -1), axes, 0, 0, tiled=True).sum(0)
    spread = jnp.broadcast_to(parts[None], (count,) + parts.shape)
    return lax.all_to_all(spread, axes, 0, 0, tiled=True).reshape(-1)


def shards(inflow_field, kernel_one, kernel_two, turbine_mask, wind_sector, wake_cotangent):
    groups, channels, height, extent = inflow_field.shape
    local_width = groups * channels
    blocks = lax.axis_size("orient")
    span = extent // blocks
    scale_factor = 1.0 / math.sqrt(G * height * lax.axis_size("strip") * extent)
    sector = wind_sector[0]
    rel_one = relation_of(sector)
    rel_two = relation_of(jnp.int32(0))
    w_one = forward_matrix(kernel_one, rel_one)
    w_two = forward_matrix(kernel_two, rel_two)
    wt_two = backward_matrix(kernel_two, rel_two)

    open_cells = (1 - turbine_mask).astype(jnp.bfloat16)[None]
    stacked = jnp.concatenate(
        [
            inflow_field.reshape(local_width, height, extent),
            wake_cotangent.reshape(local_width, height, extent),
            open_cells,
        ],
        axis=0,
    )
    widened = row_halo(stacked, 2)
    widened = jnp.pad(widened, ((0, 0), (0, 0), (2, 2)))
    mine = lax.axis_index("orient")
    open_here = lax.dynamic_slice_in_dim(widened[2 * local_width :], mine * span, span + 4, axis=2)
    open_here = open_here[0].astype(jnp.float32)
    sending = jnp.stack(
        [widened[: 2 * local_width, :, j * span : j * span + span + 4] for j in range(blocks)], 0
    )
    arrived = lax.all_to_all(sending, "orient", 0, 0, tiled=True)
    full_width = blocks * local_width
    grid_rows, grid_cols = height + 4, span + 4
    source = arrived[:, :local_width].reshape(full_width, grid_rows, grid_cols)
    cotangent = arrived[:, local_width:].reshape(full_width, grid_rows, grid_cols)

    stride = grid_cols
    flat_source = jnp.pad(source.reshape(full_width, -1), ((0, 0), (0, 2)))
    flat_cot = cotangent.reshape(full_width, -1)
    rim_len = (height + 2) * stride
    mid_len = height * stride
    live = (jnp.arange(stride) < span).astype(jnp.float32)
    open_rim = jnp.pad(open_here[1:-1, 1:-1], ((0, 0), (0, 2))).reshape(1, -1)
    open_mid = (jnp.pad(open_here[2:-2, 2:-2], ((0, 0), (0, 4)))).reshape(1, -1)
    live_mid = jnp.broadcast_to(live[None], (height, stride)).reshape(1, -1)

    x_cols = flat_windows(flat_source, [a * stride + b for a, b in TAPS], rim_len)
    first_pre = jnp.dot(w_one, x_cols, preferred_element_type=jnp.float32)
    sigmoid_one = jax.nn.sigmoid(first_pre)
    hidden = (first_pre * sigmoid_one * open_rim).astype(jnp.bfloat16)

    flat_hidden = jnp.pad(hidden, ((0, 0), (0, 2)))
    h_cols = flat_windows(flat_hidden, [a * stride + b for a, b in TAPS], mid_len)
    second_pre = jnp.dot(w_two, h_cols, preferred_element_type=jnp.float32)
    wake = second_pre.astype(jnp.bfloat16).reshape(blocks, local_width, mid_len)
    back = lax.all_to_all(wake, "orient", 0, 0, tiled=True)
    back = back.reshape(blocks, local_width, height, stride)[:, :, :, :span]
    wake_out = back.transpose(1, 2, 0, 3).reshape(groups, channels, height, extent)

    c_cols = flat_windows(flat_cot, [(3 - a) * stride + 3 - b for a, b in TAPS], mid_len)
    back_grad = jnp.dot(wt_two, c_cols, preferred_element_type=jnp.float32)
    pre_mid = first_pre[:, stride + 1 : stride + 1 + mid_len]
    sig_mid = sigmoid_one[:, stride + 1 : stride + 1 + mid_len]
    first_grad = (back_grad * open_mid * sig_mid * (1.0 + pre_mid * (1.0 - sig_mid))).astype(
        jnp.bfloat16
    )
    cot_mid = flat_cot[:, 2 * stride + 2 : 2 * stride + 2 + mid_len] * live_mid.astype(jnp.bfloat16)
    grad_two = lax.dot_general(
        cot_mid, h_cols, (((1,), (1,)), ((), ())), preferred_element_type=jnp.float32
    )
    x_mid = x_cols[:, stride + 1 : stride + 1 + mid_len]
    grad_one = lax.dot_general(
        first_grad, x_mid, (((1,), (1,)), ((), ())), preferred_element_type=jnp.float32
    )
    share_one = fold(grad_one, rel_one, channels) * scale_factor
    share_two = fold(grad_two, rel_two, channels) * scale_factor
    flat = jnp.concatenate([share_one.reshape(-1), share_two.reshape(-1)])
    flat = all_sum(flat, ("orient", "strip"))
    summed_one, summed_two = jnp.split(flat, 2)
    return (wake_out, summed_one.reshape(share_one.shape), summed_two.reshape(share_two.shape))


def solution(mesh):
    return jax.shard_map(
        shards,
        mesh=mesh,
        in_specs=(
            P("orient", None, "strip", None),
            P(),
            P(),
            P("strip", None),
            P(),
            P("orient", None, "strip", None),
        ),
        out_specs=(P("orient", None, "strip", None), P(), P()),
        check_vma=False,
    )
```

```python
import math

import jax
import jax.numpy as jnp
from jax import lax
from jax.sharding import PartitionSpec as P

G = 32
TAPS = ((0, 0), (0, 1), (0, 2), (1, 0), (1, 1), (1, 2), (2, 0), (2, 1), (2, 2))


def relative(row_ids, col_ids, sector):
    halfway = G // 2
    row_rot = row_ids % halfway
    row_ref = row_ids // halfway
    col_rot = col_ids % halfway
    col_ref = col_ids // halfway
    sec_rot = sector % halfway
    sec_ref = sector // halfway
    moved_rot = (sec_rot + (1 - 2 * sec_ref) * col_rot) % halfway
    moved_ref = (sec_ref + col_ref) % 2
    inverse_rot = jnp.where(row_ref == 0, (halfway - row_rot) % halfway, row_rot)
    result_rot = (inverse_rot + (1 - 2 * row_ref) * moved_rot) % halfway
    result_ref = (row_ref + moved_ref) % 2
    return result_ref * halfway + result_rot


def relation_of(sector):
    ids = jnp.arange(G, dtype=jnp.int32)
    return relative(ids[:, None], ids[None, :], sector).reshape(-1)


def spread_onehot(relation, channels):
    rel = relation.reshape(G, 1, 1, G, 1)
    ids = jnp.arange(G, dtype=jnp.int32).reshape(1, G, 1, 1, 1)
    c_in = jnp.arange(channels, dtype=jnp.int32).reshape(1, 1, channels, 1, 1)
    c_out = jnp.arange(channels, dtype=jnp.int32).reshape(1, 1, 1, 1, channels)
    hit = (rel == ids) & (c_in == c_out)
    return hit.astype(jnp.bfloat16).reshape(G, G * channels, G * channels)


def tap_matrix(kernel_rows, spread):
    taps = len(TAPS)
    channels = kernel_rows.shape[0] // taps
    picked = jnp.einsum("mn,gnq->gmq", kernel_rows, spread, preferred_element_type=jnp.float32)
    picked = picked.astype(jnp.bfloat16).reshape(G, taps, channels, -1)
    return picked.transpose(0, 2, 1, 3).reshape(G * channels, -1)


def fold(flat_grad, spread, channels):
    taps = len(TAPS)
    arranged = flat_grad.reshape(G, channels, taps, -1)
    folded = jnp.einsum(
        "gckn,gmn->kcm", arranged, spread.astype(jnp.float32), precision=lax.Precision.HIGHEST,
        preferred_element_type=jnp.float32,
    )
    return folded.reshape(taps, channels, G, channels).transpose(2, 0, 1, 3)


def flat_windows(flat, starts, length):
    return jnp.concatenate([flat[:, start : start + length] for start in starts], axis=0)


def row_halo(block, width):
    count = lax.axis_size("strip")
    up = [(i, i + 1) for i in range(count - 1)]
    down = [(j, i) for i, j in up]
    length = block.shape[1]
    before = lax.ppermute(block[:, length - width :], "strip", up)
    after = lax.ppermute(block[:, :width], "strip", down)
    return jnp.concatenate([before, block, after], axis=1)


def all_sum(flat, axes):
    count = lax.axis_size(axes)
    parts = lax.all_to_all(flat.reshape(count, -1), axes, 0, 0, tiled=True).sum(0)
    spread = jnp.broadcast_to(parts[None], (count,) + parts.shape)
    return lax.all_to_all(spread, axes, 0, 0, tiled=True).reshape(-1)


def shards(inflow_field, kernel_one, kernel_two, turbine_mask, wind_sector, wake_cotangent):
    groups, channels, height, extent = inflow_field.shape
    local_width = groups * channels
    blocks = lax.axis_size("orient")
    span = extent // blocks
    scale_factor = 1.0 / math.sqrt(G * height * lax.axis_size("strip") * extent)
    sector = wind_sector[0]
    rel_one = relation_of(sector)
    rel_two = relation_of(jnp.int32(0))
    spread_one = spread_onehot(rel_one, channels)
    spread_two = spread_onehot(rel_two, channels)
    spread_turned = spread_onehot(rel_two.reshape(G, G).T.reshape(-1), channels)
    taps = len(TAPS)
    w_one = tap_matrix(kernel_one.transpose(1, 2, 0, 3).reshape(taps * channels, -1), spread_one)
    w_two = tap_matrix(kernel_two.transpose(1, 2, 0, 3).reshape(taps * channels, -1), spread_two)
    wt_two = tap_matrix(
        kernel_two.transpose(1, 3, 0, 2).reshape(taps * channels, -1), spread_turned
    )

    open_cells = (1 - turbine_mask).astype(jnp.bfloat16)[None]
    stacked = jnp.concatenate(
        [
            inflow_field.reshape(local_width, height, extent),
            wake_cotangent.reshape(local_width, height, extent),
            open_cells,
        ],
        axis=0,
    )
    widened = row_halo(stacked, 2)
    widened = jnp.pad(widened, ((0, 0), (0, 0), (2, 2)))
    mine = lax.axis_index("orient")
    open_here = lax.dynamic_slice_in_dim(widened[2 * local_width :], mine * span, span + 4, axis=2)
    open_here = open_here[0].astype(jnp.float32)
    sending = jnp.stack(
        [widened[: 2 * local_width, :, j * span : j * span + span + 4] for j in range(blocks)], 0
    )
    arrived = lax.all_to_all(sending, "orient", 0, 0, tiled=True)
    full_width = blocks * local_width
    grid_rows, grid_cols = height + 4, span + 4
    source = arrived[:, :local_width].reshape(full_width, grid_rows, grid_cols)
    cotangent = arrived[:, local_width:].reshape(full_width, grid_rows, grid_cols)

    stride = grid_cols
    flat_source = jnp.pad(source.reshape(full_width, -1), ((0, 0), (0, 2)))
    flat_cot = cotangent.reshape(full_width, -1)
    rim_len = (height + 2) * stride
    mid_len = height * stride
    live = (jnp.arange(stride) < span).astype(jnp.float32)
    open_rim = jnp.pad(open_here[1:-1, 1:-1], ((0, 0), (0, 2))).reshape(1, -1)
    open_mid = (jnp.pad(open_here[2:-2, 2:-2], ((0, 0), (0, 4)))).reshape(1, -1)
    live_mid = jnp.broadcast_to(live[None], (height, stride)).reshape(1, -1)

    x_cols = flat_windows(flat_source, [a * stride + b for a, b in TAPS], rim_len)
    first_pre = jnp.dot(w_one, x_cols, preferred_element_type=jnp.float32)
    sigmoid_one = jax.nn.sigmoid(first_pre)
    hidden = (first_pre * sigmoid_one * open_rim).astype(jnp.bfloat16)

    flat_hidden = jnp.pad(hidden, ((0, 0), (0, 2)))
    h_cols = flat_windows(flat_hidden, [a * stride + b for a, b in TAPS], mid_len)
    second_pre = jnp.dot(w_two, h_cols, preferred_element_type=jnp.float32)
    wake = second_pre.reshape(full_width, height, stride)[:, :, :span].astype(jnp.bfloat16)
    wake = wake.reshape(blocks, local_width, height, span)
    back = lax.all_to_all(wake, "orient", 0, 0, tiled=True)
    wake_out = back.transpose(1, 2, 0, 3).reshape(groups, channels, height, extent)

    c_cols = flat_windows(flat_cot, [(3 - a) * stride + 3 - b for a, b in TAPS], mid_len)
    back_grad = jnp.dot(wt_two, c_cols, preferred_element_type=jnp.float32)
    pre_mid = first_pre[:, stride + 1 : stride + 1 + mid_len]
    sig_mid = sigmoid_one[:, stride + 1 : stride + 1 + mid_len]
    first_grad = (back_grad * open_mid * sig_mid * (1.0 + pre_mid * (1.0 - sig_mid))).astype(
        jnp.bfloat16
    )
    cot_mid = flat_cot[:, 2 * stride + 2 : 2 * stride + 2 + mid_len] * live_mid.astype(jnp.bfloat16)
    grad_two = lax.dot_general(
        cot_mid, h_cols, (((1,), (1,)), ((), ())), preferred_element_type=jnp.float32
    )
    x_mid = x_cols[:, stride + 1 : stride + 1 + mid_len]
    grad_one = lax.dot_general(
        first_grad, x_mid, (((1,), (1,)), ((), ())), preferred_element_type=jnp.float32
    )
    share_one = fold(grad_one, spread_one, channels) * scale_factor
    share_two = fold(grad_two, spread_two, channels) * scale_factor
    flat = jnp.concatenate([share_one.reshape(-1), share_two.reshape(-1)])
    flat = all_sum(flat, ("orient", "strip"))
    summed_one, summed_two = jnp.split(flat, 2)
    return (wake_out, summed_one.reshape(share_one.shape), summed_two.reshape(share_two.shape))


def solution(mesh):
    return jax.shard_map(
        shards,
        mesh=mesh,
        in_specs=(
            P("orient", None, "strip", None),
            P(),
            P(),
            P("strip", None),
            P(),
            P("orient", None, "strip", None),
        ),
        out_specs=(P("orient", None, "strip", None), P(), P()),
        check_vma=False,
    )
```

```python
import math

import jax
import jax.numpy as jnp
from jax import lax
from jax.sharding import PartitionSpec as P

G = 32
TAPS = ((0, 0), (0, 1), (0, 2), (1, 0), (1, 1), (1, 2), (2, 0), (2, 1), (2, 2))


def relative(row_ids, col_ids, sector):
    halfway = G // 2
    row_rot = row_ids % halfway
    row_ref = row_ids // halfway
    col_rot = col_ids % halfway
    col_ref = col_ids // halfway
    sec_rot = sector % halfway
    sec_ref = sector // halfway
    moved_rot = (sec_rot + (1 - 2 * sec_ref) * col_rot) % halfway
    moved_ref = (sec_ref + col_ref) % 2
    inverse_rot = jnp.where(row_ref == 0, (halfway - row_rot) % halfway, row_rot)
    result_rot = (inverse_rot + (1 - 2 * row_ref) * moved_rot) % halfway
    result_ref = (row_ref + moved_ref) % 2
    return result_ref * halfway + result_rot


def relation_of(sector):
    ids = jnp.arange(G, dtype=jnp.int32)
    return relative(ids[:, None], ids[None, :], sector).reshape(-1)


def forward_matrix(kernel, relation):
    taps, channels = kernel.shape[1], kernel.shape[2]
    onehot = (relation[:, None] == jnp.arange(G, dtype=jnp.int32)[None, :]).astype(kernel.dtype)
    moved = kernel.transpose(2, 0, 1, 3).reshape(channels, G, taps * channels)
    picked = jnp.einsum("xr,crm->cxm", onehot, moved, preferred_element_type=jnp.float32)
    picked = picked.astype(kernel.dtype).reshape(channels, G, G, taps * channels)
    return picked.transpose(1, 0, 2, 3).reshape(G * channels, -1)


def backward_matrix(kernel, relation):
    taps, channels = kernel.shape[1], kernel.shape[2]
    turned = relation.reshape(G, G).T.reshape(-1)
    onehot = (turned[:, None] == jnp.arange(G, dtype=jnp.int32)[None, :]).astype(kernel.dtype)
    moved = kernel.transpose(3, 0, 1, 2).reshape(channels, G, taps * channels)
    picked = jnp.einsum("xr,drm->dxm", onehot, moved, preferred_element_type=jnp.float32)
    picked = picked.astype(kernel.dtype).reshape(channels, G, G, taps * channels)
    return picked.transpose(1, 0, 2, 3).reshape(G * channels, -1)


def fold(flat_grad, relation, channels):
    taps = len(TAPS)
    arranged = flat_grad.reshape(G, channels, G, taps * channels).transpose(1, 0, 2, 3)
    arranged = arranged.reshape(channels, G * G, taps * channels)
    onehot = (relation[:, None] == jnp.arange(G, dtype=jnp.int32)[None, :]).astype(jnp.float32)
    folded = jnp.einsum(
        "xr,cxm->crm", onehot, arranged, precision=lax.Precision.HIGHEST,
        preferred_element_type=jnp.float32,
    )
    return folded.reshape(channels, G, taps, channels).transpose(1, 2, 0, 3)


def windows(grid, height, extent, start=0):
    channels = grid.shape[0] // G
    pieces = [
        grid[:, start + a : start + a + height, start + b : start + b + extent].reshape(G, channels, -1)
        for a, b in TAPS
    ]
    return jnp.stack(pieces, axis=1).reshape(grid.shape[0] * len(TAPS), -1)


def flat_windows(flat, starts, length):
    channels = flat.shape[0] // G
    pieces = [flat[:, start : start + length].reshape(G, channels, length) for start in starts]
    return jnp.stack(pieces, axis=1).reshape(flat.shape[0] * len(TAPS), length)


def row_halo(block, width):
    count = lax.axis_size("strip")
    up = [(i, i + 1) for i in range(count - 1)]
    down = [(j, i) for i, j in up]
    length = block.shape[1]
    before = lax.ppermute(block[:, length - width :], "strip", up)
    after = lax.ppermute(block[:, :width], "strip", down)
    return jnp.concatenate([before, block, after], axis=1)


def all_sum(flat, axes):
    count = lax.axis_size(axes)
    parts = lax.all_to_all(flat.reshape(count, -1), axes, 0, 0, tiled=True).sum(0)
    spread = jnp.broadcast_to(parts[None], (count,) + parts.shape)
    return lax.all_to_all(spread, axes, 0, 0, tiled=True).reshape(-1)


def shards(inflow_field, kernel_one, kernel_two, turbine_mask, wind_sector, wake_cotangent):
    groups, channels, height, extent = inflow_field.shape
    local_width = groups * channels
    blocks = lax.axis_size("orient")
    span = extent // blocks
    scale_factor = 1.0 / math.sqrt(G * height * lax.axis_size("strip") * extent)
    sector = wind_sector[0]
    rel_one = relation_of(sector)
    rel_two = relation_of(jnp.int32(0))
    w_one = forward_matrix(kernel_one, rel_one)
    w_two = forward_matrix(kernel_two, rel_two)

    open_cells = (1 - turbine_mask).astype(jnp.bfloat16)[None]
    stacked = jnp.concatenate(
        [
            inflow_field.reshape(local_width, height, extent),
            wake_cotangent.reshape(local_width, height, extent),
            open_cells,
        ],
        axis=0,
    )
    widened = row_halo(stacked, 2)
    widened = jnp.pad(widened, ((0, 0), (0, 0), (2, 2)))
    mine = lax.axis_index("orient")
    open_here = lax.dynamic_slice_in_dim(widened[2 * local_width :], mine * span, span + 4, axis=2)
    open_here = open_here[0].astype(jnp.float32)
    sending = jnp.stack(
        [widened[: 2 * local_width, :, j * span : j * span + span + 4] for j in range(blocks)], 0
    )
    arrived = lax.all_to_all(sending, "orient", 0, 0, tiled=True)
    full_width = blocks * local_width
    grid_rows, grid_cols = height + 4, span + 4
    source = arrived[:, :local_width].reshape(full_width, grid_rows, grid_cols)
    cotangent = arrived[:, local_width:].reshape(full_width, grid_rows, grid_cols)

    stride = grid_cols
    flat_source = jnp.pad(source.reshape(full_width, -1), ((0, 0), (0, 2)))
    flat_cot = cotangent.reshape(full_width, -1)
    rim_len = (height + 2) * stride
    mid_len = height * stride
    live = (jnp.arange(stride) < span).astype(jnp.float32)
    open_rim = jnp.pad(open_here[1:-1, 1:-1], ((0, 0), (0, 2))).reshape(1, -1)
    open_mid = (jnp.pad(open_here[2:-2, 2:-2], ((0, 0), (0, 4)))).reshape(1, -1)
    live_mid = jnp.broadcast_to(live[None], (height, stride)).reshape(1, -1)

    x_cols = flat_windows(flat_source, [a * stride + b for a, b in TAPS], rim_len)
    first_pre = jnp.dot(w_one, x_cols, preferred_element_type=jnp.float32)
    sigmoid_one = jax.nn.sigmoid(first_pre)
    hidden = (first_pre * sigmoid_one * open_rim).astype(jnp.bfloat16)

    flat_hidden = jnp.pad(hidden, ((0, 0), (0, 2)))
    h_cols = flat_windows(flat_hidden, [a * stride + b for a, b in TAPS], mid_len)
    second_pre = jnp.dot(w_two, h_cols, preferred_element_type=jnp.float32)
    wake = second_pre.reshape(full_width, height, stride)[:, :, :span].astype(jnp.bfloat16)
    wake = wake.reshape(blocks, local_width, height, span)
    back = lax.all_to_all(wake, "orient", 0, 0, tiled=True)
    wake_out = back.transpose(1, 2, 0, 3).reshape(groups, channels, height, extent)

    per_tap = lax.dot_general(
        w_two, flat_cot, (((0,), (0,)), ((), ())), preferred_element_type=jnp.float32
    )
    per_tap = per_tap.reshape(G, len(TAPS), channels, -1)
    back_grad = per_tap[:, 0, :, 0:mid_len] * 0.0
    for index, (a, b) in enumerate(TAPS):
        start = (3 - a) * stride + 3 - b
        back_grad = back_grad + per_tap[:, index, :, start : start + mid_len]
    back_grad = back_grad.reshape(full_width, mid_len)
    pre_mid = first_pre[:, stride + 1 : stride + 1 + mid_len]
    sig_mid = sigmoid_one[:, stride + 1 : stride + 1 + mid_len]
    first_grad = (back_grad * open_mid * sig_mid * (1.0 + pre_mid * (1.0 - sig_mid))).astype(
        jnp.bfloat16
    )
    cot_mid = flat_cot[:, 2 * stride + 2 : 2 * stride + 2 + mid_len] * live_mid.astype(jnp.bfloat16)
    grad_two = lax.dot_general(
        cot_mid, h_cols, (((1,), (1,)), ((), ())), preferred_element_type=jnp.float32
    )
    x_mid = x_cols[:, stride + 1 : stride + 1 + mid_len]
    grad_one = lax.dot_general(
        first_grad, x_mid, (((1,), (1,)), ((), ())), preferred_element_type=jnp.float32
    )
    share_one = fold(grad_one, rel_one, channels) * scale_factor
    share_two = fold(grad_two, rel_two, channels) * scale_factor
    flat = jnp.concatenate([share_one.reshape(-1), share_two.reshape(-1)])
    flat = all_sum(flat, ("orient", "strip"))
    summed_one, summed_two = jnp.split(flat, 2)
    return (wake_out, summed_one.reshape(share_one.shape), summed_two.reshape(share_two.shape))


def solution(mesh):
    return jax.shard_map(
        shards,
        mesh=mesh,
        in_specs=(
            P("orient", None, "strip", None),
            P(),
            P(),
            P("strip", None),
            P(),
            P("orient", None, "strip", None),
        ),
        out_specs=(P("orient", None, "strip", None), P(), P()),
        check_vma=False,
    )
```

```python
import math

import jax
import jax.numpy as jnp
from jax import lax
from jax.sharding import PartitionSpec as P

G = 32
TAPS = ((0, 0), (0, 1), (0, 2), (1, 0), (1, 1), (1, 2), (2, 0), (2, 1), (2, 2))


def relative(row_ids, col_ids, sector):
    halfway = G // 2
    row_rot = row_ids % halfway
    row_ref = row_ids // halfway
    col_rot = col_ids % halfway
    col_ref = col_ids // halfway
    sec_rot = sector % halfway
    sec_ref = sector // halfway
    moved_rot = (sec_rot + (1 - 2 * sec_ref) * col_rot) % halfway
    moved_ref = (sec_ref + col_ref) % 2
    inverse_rot = jnp.where(row_ref == 0, (halfway - row_rot) % halfway, row_rot)
    result_rot = (inverse_rot + (1 - 2 * row_ref) * moved_rot) % halfway
    result_ref = (row_ref + moved_ref) % 2
    return result_ref * halfway + result_rot


def relation_of(sector):
    ids = jnp.arange(G, dtype=jnp.int32)
    return relative(ids[:, None], ids[None, :], sector).reshape(-1)


def forward_matrix(kernel, relation):
    taps, channels = kernel.shape[1], kernel.shape[2]
    onehot = (relation[:, None] == jnp.arange(G, dtype=jnp.int32)[None, :]).astype(kernel.dtype)
    moved = kernel.transpose(2, 0, 1, 3).reshape(channels, G, taps * channels)
    picked = jnp.einsum("xr,crm->cxm", onehot, moved, preferred_element_type=jnp.float32)
    picked = picked.astype(kernel.dtype).reshape(channels, G, G, taps * channels)
    return picked.transpose(1, 0, 2, 3).reshape(G * channels, -1)


def backward_matrix(kernel, relation):
    taps, channels = kernel.shape[1], kernel.shape[2]
    turned = relation.reshape(G, G).T.reshape(-1)
    onehot = (turned[:, None] == jnp.arange(G, dtype=jnp.int32)[None, :]).astype(kernel.dtype)
    moved = kernel.transpose(3, 0, 1, 2).reshape(channels, G, taps * channels)
    picked = jnp.einsum("xr,drm->dxm", onehot, moved, preferred_element_type=jnp.float32)
    picked = picked.astype(kernel.dtype).reshape(channels, G, G, taps * channels)
    return picked.transpose(1, 0, 2, 3).reshape(G * channels, -1)


def fold(flat_grad, relation, channels):
    taps = len(TAPS)
    arranged = flat_grad.reshape(G, channels, G, taps * channels).transpose(1, 0, 2, 3)
    arranged = arranged.reshape(channels, G * G, taps * channels)
    onehot = (relation[:, None] == jnp.arange(G, dtype=jnp.int32)[None, :]).astype(jnp.float32)
    folded = jnp.einsum(
        "xr,cxm->crm", onehot, arranged, precision=lax.Precision.HIGHEST,
        preferred_element_type=jnp.float32,
    )
    return folded.reshape(channels, G, taps, channels).transpose(1, 2, 0, 3)


def windows(grid, height, extent, start=0):
    channels = grid.shape[0] // G
    pieces = [
        grid[:, start + a : start + a + height, start + b : start + b + extent].reshape(G, channels, -1)
        for a, b in TAPS
    ]
    return jnp.stack(pieces, axis=1).reshape(grid.shape[0] * len(TAPS), -1)


def flat_windows(flat, starts, length):
    channels = flat.shape[0] // G
    pieces = [flat[:, start : start + length].reshape(G, channels, length) for start in starts]
    return jnp.stack(pieces, axis=1).reshape(flat.shape[0] * len(TAPS), length)


def row_halo(block, width):
    count = lax.axis_size("strip")
    up = [(i, i + 1) for i in range(count - 1)]
    down = [(j, i) for i, j in up]
    length = block.shape[1]
    before = lax.ppermute(block[:, length - width :], "strip", up)
    after = lax.ppermute(block[:, :width], "strip", down)
    return jnp.concatenate([before, block, after], axis=1)


def all_sum(flat, axes):
    count = lax.axis_size(axes)
    parts = lax.all_to_all(flat.reshape(count, -1), axes, 0, 0, tiled=True).sum(0)
    spread = jnp.broadcast_to(parts[None], (count,) + parts.shape)
    return lax.all_to_all(spread, axes, 0, 0, tiled=True).reshape(-1)


def shards(inflow_field, kernel_one, kernel_two, turbine_mask, wind_sector, wake_cotangent):
    groups, channels, height, extent = inflow_field.shape
    local_width = groups * channels
    blocks = lax.axis_size("orient")
    span = extent // blocks
    scale_factor = 1.0 / math.sqrt(G * height * lax.axis_size("strip") * extent)
    sector = wind_sector[0]
    rel_one = relation_of(sector)
    rel_two = relation_of(jnp.int32(0))
    w_one = forward_matrix(kernel_one, rel_one)
    w_two = forward_matrix(kernel_two, rel_two)
    wt_two = backward_matrix(kernel_two, rel_two)

    open_cells = (1 - turbine_mask).astype(jnp.bfloat16)[None]
    stacked = jnp.concatenate(
        [
            inflow_field.reshape(local_width, height, extent),
            wake_cotangent.reshape(local_width, height, extent),
            open_cells,
        ],
        axis=0,
    )
    widened = row_halo(stacked, 2)
    widened = jnp.pad(widened, ((0, 0), (0, 0), (2, 2)))
    mine = lax.axis_index("orient")
    open_here = lax.dynamic_slice_in_dim(widened[2 * local_width :], mine * span, span + 4, axis=2)
    open_here = open_here[0].astype(jnp.float32)
    sending = jnp.stack(
        [
            widened[: 2 * local_width, :, j * span : j * span + span + 4].reshape(2 * local_width, -1)
            for j in range(blocks)
        ],
        0,
    )
    arrived = lax.all_to_all(sending, "orient", 0, 0, tiled=True)
    full_width = blocks * local_width
    grid_rows, grid_cols = height + 4, span + 4
    source = arrived[:, :local_width].reshape(full_width, grid_rows * grid_cols)
    cotangent = arrived[:, local_width:].reshape(full_width, grid_rows * grid_cols)

    stride = grid_cols
    flat_source = jnp.pad(source, ((0, 0), (0, 2)))
    flat_cot = cotangent
    rim_len = (height + 2) * stride
    mid_len = height * stride
    live = (jnp.arange(stride) < span).astype(jnp.float32)
    open_rim = jnp.pad(open_here[1:-1, 1:-1], ((0, 0), (0, 2))).reshape(1, -1)
    open_mid = (jnp.pad(open_here[2:-2, 2:-2], ((0, 0), (0, 4)))).reshape(1, -1)
    live_mid = jnp.broadcast_to(live[None], (height, stride)).reshape(1, -1)

    x_cols = flat_windows(flat_source, [a * stride + b for a, b in TAPS], rim_len)
    first_pre = jnp.dot(w_one, x_cols, preferred_element_type=jnp.float32)
    sigmoid_one = jax.nn.sigmoid(first_pre)
    hidden = (first_pre * sigmoid_one * open_rim).astype(jnp.bfloat16)

    flat_hidden = jnp.pad(hidden, ((0, 0), (0, 2)))
    h_cols = flat_windows(flat_hidden, [a * stride + b for a, b in TAPS], mid_len)
    second_pre = jnp.dot(w_two, h_cols, preferred_element_type=jnp.float32)
    wake = second_pre.reshape(full_width, height, stride)[:, :, :span].astype(jnp.bfloat16)
    wake = wake.reshape(blocks, local_width, height, span)
    back = lax.all_to_all(wake, "orient", 0, 0, tiled=True)
    wake_out = back.transpose(1, 2, 0, 3).reshape(groups, channels, height, extent)

    c_cols = flat_windows(flat_cot, [(3 - a) * stride + 3 - b for a, b in TAPS], mid_len)
    back_grad = jnp.dot(wt_two, c_cols, preferred_element_type=jnp.float32)
    pre_mid = first_pre[:, stride + 1 : stride + 1 + mid_len]
    sig_mid = sigmoid_one[:, stride + 1 : stride + 1 + mid_len]
    first_grad = (back_grad * open_mid * sig_mid * (1.0 + pre_mid * (1.0 - sig_mid))).astype(
        jnp.bfloat16
    )
    cot_mid = flat_cot[:, 2 * stride + 2 : 2 * stride + 2 + mid_len] * live_mid.astype(jnp.bfloat16)
    grad_two = lax.dot_general(
        cot_mid, h_cols, (((1,), (1,)), ((), ())), preferred_element_type=jnp.float32
    )
    x_mid = x_cols[:, stride + 1 : stride + 1 + mid_len]
    grad_one = lax.dot_general(
        first_grad, x_mid, (((1,), (1,)), ((), ())), preferred_element_type=jnp.float32
    )
    share_one = fold(grad_one, rel_one, channels) * scale_factor
    share_two = fold(grad_two, rel_two, channels) * scale_factor
    flat = jnp.concatenate([share_one.reshape(-1), share_two.reshape(-1)])
    flat = all_sum(flat, ("orient", "strip"))
    summed_one, summed_two = jnp.split(flat, 2)
    return (wake_out, summed_one.reshape(share_one.shape), summed_two.reshape(share_two.shape))


def solution(mesh):
    return jax.shard_map(
        shards,
        mesh=mesh,
        in_specs=(
            P("orient", None, "strip", None),
            P(),
            P(),
            P("strip", None),
            P(),
            P("orient", None, "strip", None),
        ),
        out_specs=(P("orient", None, "strip", None), P(), P()),
        check_vma=False,
    )
```

```python
import math

import jax
import jax.numpy as jnp
from jax import lax
from jax.sharding import PartitionSpec as P

G = 32
TAPS = ((0, 0), (0, 1), (0, 2), (1, 0), (1, 1), (1, 2), (2, 0), (2, 1), (2, 2))


def relative(row_ids, col_ids, sector):
    halfway = G // 2
    row_rot = row_ids % halfway
    row_ref = row_ids // halfway
    col_rot = col_ids % halfway
    col_ref = col_ids // halfway
    sec_rot = sector % halfway
    sec_ref = sector // halfway
    moved_rot = (sec_rot + (1 - 2 * sec_ref) * col_rot) % halfway
    moved_ref = (sec_ref + col_ref) % 2
    inverse_rot = jnp.where(row_ref == 0, (halfway - row_rot) % halfway, row_rot)
    result_rot = (inverse_rot + (1 - 2 * row_ref) * moved_rot) % halfway
    result_ref = (row_ref + moved_ref) % 2
    return result_ref * halfway + result_rot


def relation_of(sector):
    ids = jnp.arange(G, dtype=jnp.int32)
    return relative(ids[:, None], ids[None, :], sector).reshape(-1)


def forward_matrix(kernel, relation):
    taps, channels = kernel.shape[1], kernel.shape[2]
    onehot = (relation[:, None] == jnp.arange(G, dtype=jnp.int32)[None, :]).astype(kernel.dtype)
    moved = kernel.transpose(2, 0, 1, 3).reshape(channels, G, taps * channels)
    picked = jnp.einsum("xr,crm->cxm", onehot, moved, preferred_element_type=jnp.float32)
    picked = picked.astype(kernel.dtype).reshape(channels, G, G, taps * channels)
    return picked.transpose(1, 0, 2, 3).reshape(G * channels, -1)


def backward_matrix(kernel, relation):
    taps, channels = kernel.shape[1], kernel.shape[2]
    turned = relation.reshape(G, G).T.reshape(-1)
    onehot = (turned[:, None] == jnp.arange(G, dtype=jnp.int32)[None, :]).astype(kernel.dtype)
    moved = kernel.transpose(3, 0, 1, 2).reshape(channels, G, taps * channels)
    picked = jnp.einsum("xr,drm->dxm", onehot, moved, preferred_element_type=jnp.float32)
    picked = picked.astype(kernel.dtype).reshape(channels, G, G, taps * channels)
    return picked.transpose(1, 0, 2, 3).reshape(G * channels, -1)


def fold(flat_grad, relation, channels):
    taps = len(TAPS)
    arranged = flat_grad.reshape(G, channels, G, taps * channels).transpose(1, 0, 2, 3)
    arranged = arranged.reshape(channels, G * G, taps * channels)
    onehot = (relation[:, None] == jnp.arange(G, dtype=jnp.int32)[None, :]).astype(jnp.float32)
    folded = jnp.einsum(
        "xr,cxm->crm", onehot, arranged, precision=lax.Precision.HIGHEST,
        preferred_element_type=jnp.float32,
    )
    return folded.reshape(channels, G, taps, channels).transpose(1, 2, 0, 3)


def windows(grid, height, extent, start=0):
    channels = grid.shape[0] // G
    pieces = [
        grid[:, start + a : start + a + height, start + b : start + b + extent].reshape(G, channels, -1)
        for a, b in TAPS
    ]
    return jnp.stack(pieces, axis=1).reshape(grid.shape[0] * len(TAPS), -1)


def flat_windows(flat, starts, length):
    channels = flat.shape[0] // G
    pieces = [flat[:, start : start + length].reshape(G, channels, length) for start in starts]
    return jnp.stack(pieces, axis=1).reshape(flat.shape[0] * len(TAPS), length)


def row_halo(block, width):
    count = lax.axis_size("strip")
    up = [(i, i + 1) for i in range(count - 1)]
    down = [(j, i) for i, j in up]
    length = block.shape[1]
    before = lax.ppermute(block[:, length - width :], "strip", up)
    after = lax.ppermute(block[:, :width], "strip", down)
    return jnp.concatenate([before, block, after], axis=1)


def all_sum(flat, axes):
    count = lax.axis_size(axes)
    chunk = flat.shape[0] // count
    lanes = -(-chunk // 128) * 128
    pieces = jnp.pad(flat.reshape(count, chunk), ((0, 0), (0, lanes - chunk)))
    parts = lax.all_to_all(pieces, axes, 0, 0, tiled=True).sum(0)
    spread = jnp.broadcast_to(parts[None], (count, lanes))
    gathered = lax.all_to_all(spread, axes, 0, 0, tiled=True)
    return gathered[:, :chunk].reshape(-1)


def shards(inflow_field, kernel_one, kernel_two, turbine_mask, wind_sector, wake_cotangent):
    groups, channels, height, extent = inflow_field.shape
    local_width = groups * channels
    blocks = lax.axis_size("orient")
    span = extent // blocks
    scale_factor = 1.0 / math.sqrt(G * height * lax.axis_size("strip") * extent)
    sector = wind_sector[0]
    rel_one = relation_of(sector)
    rel_two = relation_of(jnp.int32(0))
    w_one = forward_matrix(kernel_one, rel_one)
    w_two = forward_matrix(kernel_two, rel_two)
    wt_two = backward_matrix(kernel_two, rel_two)

    open_cells = (1 - turbine_mask).astype(jnp.bfloat16)[None]
    stacked = jnp.concatenate(
        [
            inflow_field.reshape(local_width, height, extent),
            wake_cotangent.reshape(local_width, height, extent),
            open_cells,
        ],
        axis=0,
    )
    widened = row_halo(stacked, 2)
    widened = jnp.pad(widened, ((0, 0), (0, 0), (2, 2)))
    mine = lax.axis_index("orient")
    open_here = lax.dynamic_slice_in_dim(widened[2 * local_width :], mine * span, span + 4, axis=2)
    open_here = open_here[0].astype(jnp.float32)
    sending = jnp.stack(
        [widened[: 2 * local_width, :, j * span : j * span + span + 4] for j in range(blocks)], 0
    )
    arrived = lax.all_to_all(sending, "orient", 0, 0, tiled=True)
    full_width = blocks * local_width
    grid_rows, grid_cols = height + 4, span + 4
    source = arrived[:, :local_width].reshape(full_width, grid_rows, grid_cols)
    cotangent = arrived[:, local_width:].reshape(full_width, grid_rows, grid_cols)

    stride = grid_cols
    flat_source = jnp.pad(source.reshape(full_width, -1), ((0, 0), (0, 2)))
    flat_cot = cotangent.reshape(full_width, -1)
    rim_len = (height + 2) * stride
    mid_len = height * stride
    live = (jnp.arange(stride) < span).astype(jnp.float32)
    open_rim = jnp.pad(open_here[1:-1, 1:-1], ((0, 0), (0, 2))).reshape(1, -1)
    open_mid = (jnp.pad(open_here[2:-2, 2:-2], ((0, 0), (0, 4)))).reshape(1, -1)
    live_mid = jnp.broadcast_to(live[None], (height, stride)).reshape(1, -1)

    x_cols = flat_windows(flat_source, [a * stride + b for a, b in TAPS], rim_len)
    first_pre = jnp.dot(w_one, x_cols, preferred_element_type=jnp.float32)
    sigmoid_one = jax.nn.sigmoid(first_pre)
    hidden = (first_pre * sigmoid_one * open_rim).astype(jnp.bfloat16)

    flat_hidden = jnp.pad(hidden, ((0, 0), (0, 2)))
    h_cols = flat_windows(flat_hidden, [a * stride + b for a, b in TAPS], mid_len)
    second_pre = jnp.dot(w_two, h_cols, preferred_element_type=jnp.float32)
    wake = second_pre.reshape(full_width, height, stride)[:, :, :span].astype(jnp.bfloat16)
    wake = wake.reshape(blocks, local_width, height, span)
    back = lax.all_to_all(wake, "orient", 0, 0, tiled=True)
    wake_out = back.transpose(1, 2, 0, 3).reshape(groups, channels, height, extent)

    c_cols = flat_windows(flat_cot, [(3 - a) * stride + 3 - b for a, b in TAPS], mid_len)
    back_grad = jnp.dot(wt_two, c_cols, preferred_element_type=jnp.float32)
    pre_mid = first_pre[:, stride + 1 : stride + 1 + mid_len]
    sig_mid = sigmoid_one[:, stride + 1 : stride + 1 + mid_len]
    first_grad = (back_grad * open_mid * sig_mid * (1.0 + pre_mid * (1.0 - sig_mid))).astype(
        jnp.bfloat16
    )
    cot_mid = flat_cot[:, 2 * stride + 2 : 2 * stride + 2 + mid_len] * live_mid.astype(jnp.bfloat16)
    grad_two = lax.dot_general(
        cot_mid, h_cols, (((1,), (1,)), ((), ())), preferred_element_type=jnp.float32
    )
    x_mid = x_cols[:, stride + 1 : stride + 1 + mid_len]
    grad_one = lax.dot_general(
        first_grad, x_mid, (((1,), (1,)), ((), ())), preferred_element_type=jnp.float32
    )
    share_one = fold(grad_one, rel_one, channels) * scale_factor
    share_two = fold(grad_two, rel_two, channels) * scale_factor
    flat = jnp.concatenate([share_one.reshape(-1), share_two.reshape(-1)])
    flat = all_sum(flat, ("orient", "strip"))
    summed_one, summed_two = jnp.split(flat, 2)
    return (wake_out, summed_one.reshape(share_one.shape), summed_two.reshape(share_two.shape))


def solution(mesh):
    return jax.shard_map(
        shards,
        mesh=mesh,
        in_specs=(
            P("orient", None, "strip", None),
            P(),
            P(),
            P("strip", None),
            P(),
            P("orient", None, "strip", None),
        ),
        out_specs=(P("orient", None, "strip", None), P(), P()),
        check_vma=False,
    )
```

```python
import math

import jax
import jax.numpy as jnp
from jax import lax
from jax.sharding import PartitionSpec as P

G = 32
TAPS = ((0, 0), (0, 1), (0, 2), (1, 0), (1, 1), (1, 2), (2, 0), (2, 1), (2, 2))


def relative(row_ids, col_ids, sector):
    halfway = G // 2
    row_rot = row_ids % halfway
    row_ref = row_ids // halfway
    col_rot = col_ids % halfway
    col_ref = col_ids // halfway
    sec_rot = sector % halfway
    sec_ref = sector // halfway
    moved_rot = (sec_rot + (1 - 2 * sec_ref) * col_rot) % halfway
    moved_ref = (sec_ref + col_ref) % 2
    inverse_rot = jnp.where(row_ref == 0, (halfway - row_rot) % halfway, row_rot)
    result_rot = (inverse_rot + (1 - 2 * row_ref) * moved_rot) % halfway
    result_ref = (row_ref + moved_ref) % 2
    return result_ref * halfway + result_rot


def relation_of(sector):
    ids = jnp.arange(G, dtype=jnp.int32)
    return relative(ids[:, None], ids[None, :], sector).reshape(-1)


def forward_matrix(kernel, relation):
    taps, channels = kernel.shape[1], kernel.shape[2]
    onehot = (relation[:, None] == jnp.arange(G, dtype=jnp.int32)[None, :]).astype(kernel.dtype)
    moved = kernel.transpose(2, 0, 1, 3).reshape(channels, G, taps * channels)
    picked = jnp.einsum("xr,crm->cxm", onehot, moved, preferred_element_type=jnp.float32)
    picked = picked.astype(kernel.dtype).reshape(channels, G, G, taps * channels)
    return picked.transpose(1, 0, 2, 3).reshape(G * channels, -1)


def forward_pair(kernels, relations):
    pair, taps, channels = kernels.shape[0], kernels.shape[2], kernels.shape[3]
    onehot = (relations[:, :, None] == jnp.arange(G, dtype=jnp.int32)).astype(kernels.dtype)
    moved = kernels.transpose(0, 3, 1, 2, 4).reshape(pair, channels, G, taps * channels)
    picked = jnp.einsum("bxr,bcrm->bcxm", onehot, moved, preferred_element_type=jnp.float32)
    picked = picked.astype(kernels.dtype).reshape(pair, channels, G, G, taps * channels)
    return picked.transpose(0, 2, 1, 3, 4).reshape(pair, G * channels, -1)


def fold_pair(grads, relations, channels):
    pair, taps = grads.shape[0], len(TAPS)
    arranged = grads.reshape(pair, G, channels, G, taps * channels).transpose(0, 2, 1, 3, 4)
    arranged = arranged.reshape(pair, channels, G * G, taps * channels)
    onehot = (relations[:, :, None] == jnp.arange(G, dtype=jnp.int32)).astype(jnp.float32)
    folded = jnp.einsum(
        "bxr,bcxm->bcrm", onehot, arranged, precision=lax.Precision.HIGHEST,
        preferred_element_type=jnp.float32,
    )
    folded = folded.reshape(pair, channels, G, taps, channels)
    return folded.transpose(0, 2, 3, 1, 4)


def backward_matrix(kernel, relation):
    taps, channels = kernel.shape[1], kernel.shape[2]
    turned = relation.reshape(G, G).T.reshape(-1)
    onehot = (turned[:, None] == jnp.arange(G, dtype=jnp.int32)[None, :]).astype(kernel.dtype)
    moved = kernel.transpose(3, 0, 1, 2).reshape(channels, G, taps * channels)
    picked = jnp.einsum("xr,drm->dxm", onehot, moved, preferred_element_type=jnp.float32)
    picked = picked.astype(kernel.dtype).reshape(channels, G, G, taps * channels)
    return picked.transpose(1, 0, 2, 3).reshape(G * channels, -1)


def fold(flat_grad, relation, channels):
    taps = len(TAPS)
    arranged = flat_grad.reshape(G, channels, G, taps * channels).transpose(1, 0, 2, 3)
    arranged = arranged.reshape(channels, G * G, taps * channels)
    onehot = (relation[:, None] == jnp.arange(G, dtype=jnp.int32)[None, :]).astype(jnp.float32)
    folded = jnp.einsum(
        "xr,cxm->crm", onehot, arranged, precision=lax.Precision.HIGHEST,
        preferred_element_type=jnp.float32,
    )
    return folded.reshape(channels, G, taps, channels).transpose(1, 2, 0, 3)


def windows(grid, height, extent, start=0):
    channels = grid.shape[0] // G
    pieces = [
        grid[:, start + a : start + a + height, start + b : start + b + extent].reshape(G, channels, -1)
        for a, b in TAPS
    ]
    return jnp.stack(pieces, axis=1).reshape(grid.shape[0] * len(TAPS), -1)


def flat_windows(flat, starts, length):
    channels = flat.shape[0] // G
    pieces = [flat[:, start : start + length].reshape(G, channels, length) for start in starts]
    return jnp.stack(pieces, axis=1).reshape(flat.shape[0] * len(TAPS), length)


def row_halo(block, width):
    count = lax.axis_size("strip")
    up = [(i, i + 1) for i in range(count - 1)]
    down = [(j, i) for i, j in up]
    length = block.shape[1]
    before = lax.ppermute(block[:, length - width :], "strip", up)
    after = lax.ppermute(block[:, :width], "strip", down)
    return jnp.concatenate([before, block, after], axis=1)


def all_sum(flat, axes):
    count = lax.axis_size(axes)
    parts = lax.all_to_all(flat.reshape(count, -1), axes, 0, 0, tiled=True).sum(0)
    spread = jnp.broadcast_to(parts[None], (count,) + parts.shape)
    return lax.all_to_all(spread, axes, 0, 0, tiled=True).reshape(-1)


def shards(inflow_field, kernel_one, kernel_two, turbine_mask, wind_sector, wake_cotangent):
    groups, channels, height, extent = inflow_field.shape
    local_width = groups * channels
    blocks = lax.axis_size("orient")
    span = extent // blocks
    scale_factor = 1.0 / math.sqrt(G * height * lax.axis_size("strip") * extent)
    sector = wind_sector[0]
    rel_one = relation_of(sector)
    rel_two = relation_of(jnp.int32(0))
    relations = jnp.stack([rel_one, rel_two])
    pair_w = forward_pair(jnp.stack([kernel_one, kernel_two]), relations)
    w_one, w_two = pair_w[0], pair_w[1]
    wt_two = backward_matrix(kernel_two, rel_two)

    open_cells = (1 - turbine_mask).astype(jnp.bfloat16)[None]
    stacked = jnp.concatenate(
        [
            inflow_field.reshape(local_width, height, extent),
            wake_cotangent.reshape(local_width, height, extent),
            open_cells,
        ],
        axis=0,
    )
    widened = row_halo(stacked, 2)
    widened = jnp.pad(widened, ((0, 0), (0, 0), (2, 2)))
    mine = lax.axis_index("orient")
    open_here = lax.dynamic_slice_in_dim(widened[2 * local_width :], mine * span, span + 4, axis=2)
    open_here = open_here[0].astype(jnp.float32)
    sending = jnp.stack(
        [widened[: 2 * local_width, :, j * span : j * span + span + 4] for j in range(blocks)], 0
    )
    arrived = lax.all_to_all(sending, "orient", 0, 0, tiled=True)
    full_width = blocks * local_width
    grid_rows, grid_cols = height + 4, span + 4
    source = arrived[:, :local_width].reshape(full_width, grid_rows, grid_cols)
    cotangent = arrived[:, local_width:].reshape(full_width, grid_rows, grid_cols)

    stride = grid_cols
    flat_source = jnp.pad(source.reshape(full_width, -1), ((0, 0), (0, 2)))
    flat_cot = cotangent.reshape(full_width, -1)
    rim_len = (height + 2) * stride
    mid_len = height * stride
    live = (jnp.arange(stride) < span).astype(jnp.float32)
    open_rim = jnp.pad(open_here[1:-1, 1:-1], ((0, 0), (0, 2))).reshape(1, -1)
    open_mid = (jnp.pad(open_here[2:-2, 2:-2], ((0, 0), (0, 4)))).reshape(1, -1)
    live_mid = jnp.broadcast_to(live[None], (height, stride)).reshape(1, -1)

    x_cols = flat_windows(flat_source, [a * stride + b for a, b in TAPS], rim_len)
    first_pre = jnp.dot(w_one, x_cols, preferred_element_type=jnp.float32)
    sigmoid_one = jax.nn.sigmoid(first_pre)
    hidden = (first_pre * sigmoid_one * open_rim).astype(jnp.bfloat16)

    flat_hidden = jnp.pad(hidden, ((0, 0), (0, 2)))
    h_cols = flat_windows(flat_hidden, [a * stride + b for a, b in TAPS], mid_len)
    second_pre = jnp.dot(w_two, h_cols, preferred_element_type=jnp.float32)
    wake = second_pre.reshape(full_width, height, stride)[:, :, :span].astype(jnp.bfloat16)
    wake = wake.reshape(blocks, local_width, height, span)
    back = lax.all_to_all(wake, "orient", 0, 0, tiled=True)
    wake_out = back.transpose(1, 2, 0, 3).reshape(groups, channels, height, extent)

    c_cols = flat_windows(flat_cot, [(3 - a) * stride + 3 - b for a, b in TAPS], mid_len)
    back_grad = jnp.dot(wt_two, c_cols, preferred_element_type=jnp.float32)
    pre_mid = first_pre[:, stride + 1 : stride + 1 + mid_len]
    sig_mid = sigmoid_one[:, stride + 1 : stride + 1 + mid_len]
    first_grad = (back_grad * open_mid * sig_mid * (1.0 + pre_mid * (1.0 - sig_mid))).astype(
        jnp.bfloat16
    )
    cot_mid = flat_cot[:, 2 * stride + 2 : 2 * stride + 2 + mid_len] * live_mid.astype(jnp.bfloat16)
    grad_two = lax.dot_general(
        cot_mid, h_cols, (((1,), (1,)), ((), ())), preferred_element_type=jnp.float32
    )
    x_mid = x_cols[:, stride + 1 : stride + 1 + mid_len]
    grad_one = lax.dot_general(
        first_grad, x_mid, (((1,), (1,)), ((), ())), preferred_element_type=jnp.float32
    )
    shares = fold_pair(jnp.stack([grad_one, grad_two]), relations, channels) * scale_factor
    flat = all_sum(shares.reshape(-1), ("orient", "strip"))
    summed = flat.reshape(shares.shape)
    return (wake_out, summed[0], summed[1])


def solution(mesh):
    return jax.shard_map(
        shards,
        mesh=mesh,
        in_specs=(
            P("orient", None, "strip", None),
            P(),
            P(),
            P("strip", None),
            P(),
            P("orient", None, "strip", None),
        ),
        out_specs=(P("orient", None, "strip", None), P(), P()),
        check_vma=False,
    )
```

```python
import math

import jax
import jax.numpy as jnp
from jax import lax
from jax.sharding import PartitionSpec as P

G = 32
TAPS = ((0, 0), (0, 1), (0, 2), (1, 0), (1, 1), (1, 2), (2, 0), (2, 1), (2, 2))


def relative(row_ids, col_ids, sector):
    halfway = G // 2
    row_rot = row_ids % halfway
    row_ref = row_ids // halfway
    col_rot = col_ids % halfway
    col_ref = col_ids // halfway
    sec_rot = sector % halfway
    sec_ref = sector // halfway
    moved_rot = (sec_rot + (1 - 2 * sec_ref) * col_rot) % halfway
    moved_ref = (sec_ref + col_ref) % 2
    inverse_rot = jnp.where(row_ref == 0, (halfway - row_rot) % halfway, row_rot)
    result_rot = (inverse_rot + (1 - 2 * row_ref) * moved_rot) % halfway
    result_ref = (row_ref + moved_ref) % 2
    return result_ref * halfway + result_rot


def relation_of(sector):
    ids = jnp.arange(G, dtype=jnp.int32)
    return relative(ids[:, None], ids[None, :], sector).reshape(-1)


def forward_matrix(kernel, relation):
    taps, channels = kernel.shape[1], kernel.shape[2]
    onehot = (relation[:, None] == jnp.arange(G, dtype=jnp.int32)[None, :]).astype(kernel.dtype)
    moved = kernel.transpose(2, 0, 1, 3).reshape(channels, G, taps * channels)
    picked = jnp.einsum("xr,crm->cxm", onehot, moved, preferred_element_type=jnp.float32)
    picked = picked.astype(kernel.dtype).reshape(channels, G, G, taps * channels)
    return picked.transpose(1, 0, 2, 3).reshape(G * channels, -1)


def backward_matrix(kernel, relation):
    taps, channels = kernel.shape[1], kernel.shape[2]
    turned = relation.reshape(G, G).T.reshape(-1)
    onehot = (turned[:, None] == jnp.arange(G, dtype=jnp.int32)[None, :]).astype(kernel.dtype)
    moved = kernel.transpose(3, 0, 1, 2).reshape(channels, G, taps * channels)
    picked = jnp.einsum("xr,drm->dxm", onehot, moved, preferred_element_type=jnp.float32)
    picked = picked.astype(kernel.dtype).reshape(channels, G, G, taps * channels)
    return picked.transpose(1, 0, 2, 3).reshape(G * channels, -1)


def fold(flat_grad, relation, channels):
    taps = len(TAPS)
    arranged = flat_grad.reshape(G, channels, G, taps * channels).transpose(1, 0, 2, 3)
    arranged = arranged.reshape(channels, G * G, taps * channels)
    onehot = (relation[:, None] == jnp.arange(G, dtype=jnp.int32)[None, :]).astype(jnp.float32)
    folded = jnp.einsum(
        "xr,cxm->crm", onehot, arranged, precision=lax.Precision.HIGHEST,
        preferred_element_type=jnp.float32,
    )
    return folded.reshape(channels, G, taps, channels).transpose(1, 2, 0, 3)


def windows(grid, height, extent, start=0):
    channels = grid.shape[0] // G
    pieces = [
        grid[:, start + a : start + a + height, start + b : start + b + extent].reshape(G, channels, -1)
        for a, b in TAPS
    ]
    return jnp.stack(pieces, axis=1).reshape(grid.shape[0] * len(TAPS), -1)


def flat_windows(flat, starts, length):
    channels = flat.shape[0] // G
    pieces = [flat[:, start : start + length].reshape(G, channels, length) for start in starts]
    return jnp.stack(pieces, axis=1).reshape(flat.shape[0] * len(TAPS), length)


def row_halo(block, width):
    count = lax.axis_size("strip")
    up = [(i, i + 1) for i in range(count - 1)]
    down = [(j, i) for i, j in up]
    length = block.shape[1]
    before = lax.ppermute(block[:, length - width :], "strip", up)
    after = lax.ppermute(block[:, :width], "strip", down)
    return jnp.concatenate([before, block, after], axis=1)


def all_sum(flat, axes):
    count = lax.axis_size(axes)
    parts = lax.all_to_all(flat.reshape(count, -1), axes, 0, 0, tiled=True).sum(0)
    spread = jnp.broadcast_to(parts[None], (count,) + parts.shape)
    return lax.all_to_all(spread, axes, 0, 0, tiled=True).reshape(-1)


def shards(inflow_field, kernel_one, kernel_two, turbine_mask, wind_sector, wake_cotangent):
    groups, channels, height, extent = inflow_field.shape
    local_width = groups * channels
    blocks = lax.axis_size("orient")
    span = extent // blocks
    scale_factor = 1.0 / math.sqrt(G * height * lax.axis_size("strip") * extent)
    sector = wind_sector[0]
    rel_one = relation_of(sector)
    rel_two = relation_of(jnp.int32(0))
    w_one = forward_matrix(kernel_one, rel_one)
    w_two = forward_matrix(kernel_two, rel_two)
    wt_two = backward_matrix(kernel_two, rel_two)

    open_cells = (1 - turbine_mask).astype(jnp.bfloat16)[None]
    stacked = jnp.concatenate(
        [
            inflow_field.reshape(local_width, height, extent),
            wake_cotangent.reshape(local_width, height, extent),
            open_cells,
        ],
        axis=0,
    )
    widened = row_halo(stacked, 2)
    widened = jnp.pad(widened, ((0, 0), (0, 0), (2, 2)))
    mine = lax.axis_index("orient")
    open_here = lax.dynamic_slice_in_dim(widened[2 * local_width :], mine * span, span + 4, axis=2)
    open_here = open_here[0].astype(jnp.float32)
    sending = jnp.stack(
        [widened[: 2 * local_width, :, j * span : j * span + span + 4] for j in range(blocks)], 0
    )
    arrived = lax.all_to_all(sending, "orient", 0, 0, tiled=True)
    full_width = blocks * local_width
    grid_rows, grid_cols = height + 4, span + 4
    source = arrived[:, :local_width].reshape(full_width, grid_rows, grid_cols)
    cotangent = arrived[:, local_width:].reshape(full_width, grid_rows, grid_cols)

    stride = grid_cols
    flat_source = jnp.pad(source.reshape(full_width, -1), ((0, 0), (0, 2)))
    flat_cot = cotangent.reshape(full_width, -1)
    rim_len = (height + 2) * stride
    mid_len = height * stride
    live = (jnp.arange(stride) < span).astype(jnp.float32)
    open_rim = jnp.pad(open_here[1:-1, 1:-1], ((0, 0), (0, 2))).reshape(1, -1)
    open_mid = (jnp.pad(open_here[2:-2, 2:-2], ((0, 0), (0, 4)))).reshape(1, -1)
    live_mid = jnp.broadcast_to(live[None], (height, stride)).reshape(1, -1)

    x_cols = flat_windows(flat_source, [a * stride + b for a, b in TAPS], rim_len)
    first_pre = jnp.dot(w_one, x_cols, preferred_element_type=jnp.float32)
    sigmoid_one = jax.nn.sigmoid(first_pre)
    hidden = (first_pre * sigmoid_one * open_rim).astype(jnp.bfloat16)

    flat_hidden = jnp.pad(hidden, ((0, 0), (0, 2)))
    h_cols = flat_windows(flat_hidden, [a * stride + b for a, b in TAPS], mid_len)
    second_pre = jnp.dot(w_two, h_cols, preferred_element_type=jnp.float32)
    wake = second_pre.reshape(full_width, height, stride)[:, :, :span].astype(jnp.bfloat16)
    wake = wake.reshape(blocks, local_width, height, span)
    back = lax.all_to_all(wake, "orient", 0, 0, tiled=True)
    wake_out = back.transpose(1, 2, 0, 3).reshape(groups, channels, height, extent)

    c_cols = flat_windows(flat_cot, [(3 - a) * stride + 3 - b for a, b in TAPS], mid_len)
    back_grad = jnp.dot(wt_two, c_cols, preferred_element_type=jnp.float32)
    pre_mid = first_pre[:, stride + 1 : stride + 1 + mid_len]
    sig_mid = sigmoid_one[:, stride + 1 : stride + 1 + mid_len]
    first_grad = (back_grad * open_mid * sig_mid * (1.0 + pre_mid * (1.0 - sig_mid))).astype(
        jnp.bfloat16
    )
    cot_mid = flat_cot[:, 2 * stride + 2 : 2 * stride + 2 + mid_len] * live_mid.astype(jnp.bfloat16)
    grad_two = lax.dot_general(
        cot_mid, h_cols, (((1,), (1,)), ((), ())), preferred_element_type=jnp.float32
    )
    x_mid = x_cols[:, stride + 1 : stride + 1 + mid_len]
    grad_one = lax.dot_general(
        first_grad, x_mid, (((1,), (1,)), ((), ())), preferred_element_type=jnp.float32
    )
    share_one = fold(grad_one, rel_one, channels) * scale_factor
    share_two = fold(grad_two, rel_two, channels) * scale_factor
    flat = jnp.concatenate([share_one.reshape(-1), share_two.reshape(-1)])
    flat, back = lax.optimization_barrier((flat, back))
    wake_out = back.transpose(1, 2, 0, 3).reshape(groups, channels, height, extent)
    flat = all_sum(flat, ("orient", "strip"))
    summed_one, summed_two = jnp.split(flat, 2)
    return (wake_out, summed_one.reshape(share_one.shape), summed_two.reshape(share_two.shape))


def solution(mesh):
    return jax.shard_map(
        shards,
        mesh=mesh,
        in_specs=(
            P("orient", None, "strip", None),
            P(),
            P(),
            P("strip", None),
            P(),
            P("orient", None, "strip", None),
        ),
        out_specs=(P("orient", None, "strip", None), P(), P()),
        check_vma=False,
    )
```

```python
import math

import jax
import jax.numpy as jnp
from jax import lax
from jax.sharding import PartitionSpec as P

G = 32
TAPS = ((0, 0), (0, 1), (0, 2), (1, 0), (1, 1), (1, 2), (2, 0), (2, 1), (2, 2))


def relative(row_ids, col_ids, sector):
    halfway = G // 2
    row_rot = row_ids % halfway
    row_ref = row_ids // halfway
    col_rot = col_ids % halfway
    col_ref = col_ids // halfway
    sec_rot = sector % halfway
    sec_ref = sector // halfway
    moved_rot = (sec_rot + (1 - 2 * sec_ref) * col_rot) % halfway
    moved_ref = (sec_ref + col_ref) % 2
    inverse_rot = jnp.where(row_ref == 0, (halfway - row_rot) % halfway, row_rot)
    result_rot = (inverse_rot + (1 - 2 * row_ref) * moved_rot) % halfway
    result_ref = (row_ref + moved_ref) % 2
    return result_ref * halfway + result_rot


def relation_of(sector):
    ids = jnp.arange(G, dtype=jnp.int32)
    return relative(ids[:, None], ids[None, :], sector).reshape(-1)


def forward_matrix(kernel, relation):
    taps, channels = kernel.shape[1], kernel.shape[2]
    onehot = (relation[:, None] == jnp.arange(G, dtype=jnp.int32)[None, :]).astype(kernel.dtype)
    moved = kernel.transpose(2, 0, 1, 3).reshape(channels, G, taps * channels)
    picked = jnp.einsum("xr,crm->cxm", onehot, moved, preferred_element_type=jnp.float32)
    picked = picked.astype(kernel.dtype).reshape(channels, G, G, taps * channels)
    return picked.transpose(1, 0, 2, 3).reshape(G * channels, -1)


def backward_matrix(kernel, relation):
    taps, channels = kernel.shape[1], kernel.shape[2]
    turned = relation.reshape(G, G).T.reshape(-1)
    onehot = (turned[:, None] == jnp.arange(G, dtype=jnp.int32)[None, :]).astype(kernel.dtype)
    moved = kernel.transpose(3, 0, 1, 2).reshape(channels, G, taps * channels)
    picked = jnp.einsum("xr,drm->dxm", onehot, moved, preferred_element_type=jnp.float32)
    picked = picked.astype(kernel.dtype).reshape(channels, G, G, taps * channels)
    return picked.transpose(1, 0, 2, 3).reshape(G * channels, -1)


def fold(flat_grad, relation, channels):
    taps = len(TAPS)
    arranged = flat_grad.reshape(G, channels, G, taps * channels).transpose(1, 0, 2, 3)
    arranged = arranged.reshape(channels, G * G, taps * channels)
    onehot = (relation[:, None] == jnp.arange(G, dtype=jnp.int32)[None, :]).astype(jnp.float32)
    folded = jnp.einsum(
        "xr,cxm->crm", onehot, arranged, precision=lax.Precision.HIGH,
        preferred_element_type=jnp.float32,
    )
    return folded.reshape(channels, G, taps, channels).transpose(1, 2, 0, 3)


def windows(grid, height, extent, start=0):
    channels = grid.shape[0] // G
    pieces = [
        grid[:, start + a : start + a + height, start + b : start + b + extent].reshape(G, channels, -1)
        for a, b in TAPS
    ]
    return jnp.stack(pieces, axis=1).reshape(grid.shape[0] * len(TAPS), -1)


def flat_windows(flat, starts, length):
    channels = flat.shape[0] // G
    pieces = [flat[:, start : start + length].reshape(G, channels, length) for start in starts]
    return jnp.stack(pieces, axis=1).reshape(flat.shape[0] * len(TAPS), length)


def row_halo(block, width):
    count = lax.axis_size("strip")
    up = [(i, i + 1) for i in range(count - 1)]
    down = [(j, i) for i, j in up]
    length = block.shape[1]
    before = lax.ppermute(block[:, length - width :], "strip", up)
    after = lax.ppermute(block[:, :width], "strip", down)
    return jnp.concatenate([before, block, after], axis=1)


def all_sum(flat, axes):
    count = lax.axis_size(axes)
    parts = lax.all_to_all(flat.reshape(count, -1), axes, 0, 0, tiled=True).sum(0)
    spread = jnp.broadcast_to(parts[None], (count,) + parts.shape)
    return lax.all_to_all(spread, axes, 0, 0, tiled=True).reshape(-1)


def shards(inflow_field, kernel_one, kernel_two, turbine_mask, wind_sector, wake_cotangent):
    groups, channels, height, extent = inflow_field.shape
    local_width = groups * channels
    blocks = lax.axis_size("orient")
    span = extent // blocks
    scale_factor = 1.0 / math.sqrt(G * height * lax.axis_size("strip") * extent)
    sector = wind_sector[0]
    rel_one = relation_of(sector)
    rel_two = relation_of(jnp.int32(0))
    w_one = forward_matrix(kernel_one, rel_one)
    w_two = forward_matrix(kernel_two, rel_two)
    wt_two = backward_matrix(kernel_two, rel_two)

    open_cells = (1 - turbine_mask).astype(jnp.bfloat16)[None]
    stacked = jnp.concatenate(
        [
            inflow_field.reshape(local_width, height, extent),
            wake_cotangent.reshape(local_width, height, extent),
            open_cells,
        ],
        axis=0,
    )
    widened = row_halo(stacked, 2)
    widened = jnp.pad(widened, ((0, 0), (0, 0), (2, 2)))
    mine = lax.axis_index("orient")
    open_here = lax.dynamic_slice_in_dim(widened[2 * local_width :], mine * span, span + 4, axis=2)
    open_here = open_here[0].astype(jnp.float32)
    sending = jnp.stack(
        [widened[: 2 * local_width, :, j * span : j * span + span + 4] for j in range(blocks)], 0
    )
    arrived = lax.all_to_all(sending, "orient", 0, 0, tiled=True)
    full_width = blocks * local_width
    grid_rows, grid_cols = height + 4, span + 4
    source = arrived[:, :local_width].reshape(full_width, grid_rows, grid_cols)
    cotangent = arrived[:, local_width:].reshape(full_width, grid_rows, grid_cols)

    stride = grid_cols
    flat_source = jnp.pad(source.reshape(full_width, -1), ((0, 0), (0, 2)))
    flat_cot = cotangent.reshape(full_width, -1)
    rim_len = (height + 2) * stride
    mid_len = height * stride
    live = (jnp.arange(stride) < span).astype(jnp.float32)
    open_rim = jnp.pad(open_here[1:-1, 1:-1], ((0, 0), (0, 2))).reshape(1, -1)
    open_mid = (jnp.pad(open_here[2:-2, 2:-2], ((0, 0), (0, 4)))).reshape(1, -1)
    live_mid = jnp.broadcast_to(live[None], (height, stride)).reshape(1, -1)

    x_cols = flat_windows(flat_source, [a * stride + b for a, b in TAPS], rim_len)
    first_pre = jnp.dot(w_one, x_cols, preferred_element_type=jnp.float32)
    sigmoid_one = jax.nn.sigmoid(first_pre)
    hidden = (first_pre * sigmoid_one * open_rim).astype(jnp.bfloat16)

    flat_hidden = jnp.pad(hidden, ((0, 0), (0, 2)))
    h_cols = flat_windows(flat_hidden, [a * stride + b for a, b in TAPS], mid_len)
    second_pre = jnp.dot(w_two, h_cols, preferred_element_type=jnp.float32)
    wake = second_pre.reshape(full_width, height, stride)[:, :, :span].astype(jnp.bfloat16)
    wake = wake.reshape(blocks, local_width, height, span)
    back = lax.all_to_all(wake, "orient", 0, 0, tiled=True)
    wake_out = back.transpose(1, 2, 0, 3).reshape(groups, channels, height, extent)

    c_cols = flat_windows(flat_cot, [(3 - a) * stride + 3 - b for a, b in TAPS], mid_len)
    back_grad = jnp.dot(wt_two, c_cols, preferred_element_type=jnp.float32)
    pre_mid = first_pre[:, stride + 1 : stride + 1 + mid_len]
    sig_mid = sigmoid_one[:, stride + 1 : stride + 1 + mid_len]
    first_grad = (back_grad * open_mid * sig_mid * (1.0 + pre_mid * (1.0 - sig_mid))).astype(
        jnp.bfloat16
    )
    cot_mid = flat_cot[:, 2 * stride + 2 : 2 * stride + 2 + mid_len] * live_mid.astype(jnp.bfloat16)
    grad_two = lax.dot_general(
        cot_mid, h_cols, (((1,), (1,)), ((), ())), preferred_element_type=jnp.float32
    )
    x_mid = x_cols[:, stride + 1 : stride + 1 + mid_len]
    grad_one = lax.dot_general(
        first_grad, x_mid, (((1,), (1,)), ((), ())), preferred_element_type=jnp.float32
    )
    share_one = fold(grad_one, rel_one, channels) * scale_factor
    share_two = fold(grad_two, rel_two, channels) * scale_factor
    flat = jnp.concatenate([share_one.reshape(-1), share_two.reshape(-1)])
    flat = all_sum(flat, ("orient", "strip"))
    summed_one, summed_two = jnp.split(flat, 2)
    return (wake_out, summed_one.reshape(share_one.shape), summed_two.reshape(share_two.shape))


def solution(mesh):
    return jax.shard_map(
        shards,
        mesh=mesh,
        in_specs=(
            P("orient", None, "strip", None),
            P(),
            P(),
            P("strip", None),
            P(),
            P("orient", None, "strip", None),
        ),
        out_specs=(P("orient", None, "strip", None), P(), P()),
        check_vma=False,
    )
```
